128 devices in a mesh: dp: 8 (over z, core), ctx: 16 (over y, x).
Axes of the slice: x: 4, y: 4, z: 4, core: 2. Of those that a mesh axis runs over, the one named last changes fastest.
Arguments:
- ids: int32 [8, 4096, 8], P('dp', 'ctx'), may hold values from 0 to 1023
- tables: bfloat16 [8, 1024, 1024], P(None, 'dp', 'ctx'), may hold values from -2.09375 to 2.09375
- w_qkv: bfloat16 [1024, 3072], P('dp'), may hold values from -5 to 5
- w_out: bfloat16 [1024, 1024], P('dp'), may hold values from -0.1875 to 0.1875
- attn_gain: float32 [1024], replicated, may hold values from 0.1 to 1.9
- conv_gain: float32 [1024], replicated, may hold values from 0.1 to 1.9
- conv_kernel: float32 [31, 1024], replicated, may hold values from -1 to 1
- back_list: int32 [16, 2], replicated, may hold values from 0 to 17, as said below
- ahead_list: int32 [16, 1], replicated, may hold values from 1 to 17, as said below
- cotangent: bfloat16 [8, 4096, 1024], P('dp', 'ctx'), may hold values from -8 to 8
Outputs:
- block_out: bfloat16 [8, 4096, 1024], P('dp', 'ctx')
- grad_embedded: bfloat16 [8, 4096, 1024], P('dp', 'ctx')
- grad_qkv: float32 [1024, 3072], P('dp')
- grad_out: float32 [1024, 1024], P('dp')
- grad_kernel: float32 [31, 1024], replicated
The draws below stay inside these ranges and needn't reach their ends.
Inputs may be any that keep to these rules, and one draw needn't show every extreme that they name: `back_list`: row b lists distinct blocks among b - 2 .. b - 1 that exist, first, then the filler 16 + 1; block 2 and the last block list all 2, the first none. `ahead_list`: row b lists distinct blocks among b + 1 .. b + 1 that exist, first, then the filler 16 + 1; block 0 lists all 1, the last none.
All inputs are finite; a program needn't handle non-finite values.
Results may differ from the reference program's by a relative error of at most 0.015.
Values may be sent and summed in bfloat16 or wider, within the bound.
No kernel may reach another device: no remote copies, remote signals or barrier semaphores. Data moves between devices by JAX's collectives and lax.ppermute only.
A program may use at most 128 MiB of HBM per device.

```python
import math
import jax
import jax.numpy as jnp
import numpy as np
from jax import lax

D = 1024
HEADS = 16
HD = 64
NCB = 8
VOCAB = 1024
KT = 31
BLOCK = 256
WB = 2
WF = 1
RECS = 8
BLOCKS = 16
FRAMES = 4096


def block_list(key, reach_count, direction, forced, second):
    blocks = jnp.arange(BLOCKS, dtype=jnp.int32)[:, None]
    slot_index = jnp.arange(reach_count, dtype=jnp.int32)[None, :]
    target = jnp.broadcast_to(blocks + direction * (1 + slot_index), (BLOCKS, reach_count))
    coin_flips = jax.random.randint(key, (BLOCKS, reach_count), 0, 2)
    forcing = ((blocks == forced) | (blocks == second)).astype(jnp.int32)
    chosen = coin_flips + forcing > 0
    chosen = chosen & (target >= 0) & (target < BLOCKS)
    ranking = jnp.where(chosen, slot_index, reach_count + slot_index)
    ordering = jnp.argsort(ranking, axis=1)
    chosen_sorted = jnp.take_along_axis(chosen, ordering, axis=1)
    target_sorted = jnp.take_along_axis(target, ordering, axis=1)
    return jnp.where(chosen_sorted, target_sorted, BLOCKS + WF).astype(jnp.int32)


def draw_back_list(key, part):
    return block_list(jax.random.fold_in(key, 11), WB, -1, BLOCKS - 1, WB)


def draw_ahead_list(key, part):
    return block_list(jax.random.fold_in(key, 13), WF, 1, 0, 0)


def draw_w_qkv(key, part):
    base = jax.random.truncated_normal(key, -4.0, 4.0, (D, 3 * D), jnp.float32) / math.sqrt(D)
    return base.astype(jnp.bfloat16)


def draw_cotangent(key, part):
    frame = jnp.arange(FRAMES, dtype=jnp.float32)
    rising = 0.5 + frame / FRAMES
    noise = jnp.clip(jax.random.normal(key, (RECS, FRAMES, D), jnp.float32), -4.0, 4.0)
    return jnp.clip(noise * rising[None, :, None], -8.0, 8.0).astype(jnp.bfloat16)


def plant(values, own_key, smallest, high):
    extent = values.shape
    place = [jax.random.randint(jax.random.fold_in(own_key, axis), (), 0, extent[axis]) for axis in range(len(extent))]
    values = values.at[tuple(place)].set(smallest)
    longest = extent.index(max(extent))
    place[longest] = (place[longest] + 1) % extent[longest]
    return values.at[tuple(place)].set(high)


def block_scale(stream_key, dims, shards, smallest, high):
    gain, own = 1.0, jax.random.fold_in(stream_key, 6)
    for dim, blocks in shards:
        heights = jnp.exp(jax.random.uniform(jax.random.fold_in(own, dim), (blocks,), jnp.float32, smallest / len(shards), high / len(shards)))
        gain = gain * jnp.repeat(heights, dims[dim] // blocks).reshape([-1 if axis == dim else 1 for axis in range(len(dims))])
    return gain


def cumulative_ranks(number_of, skew):
    loads = [(1 << 20) // math.isqrt(rank ** skew) + 1 for rank in range(1, number_of + 1)]
    deviation = 1 + sum(loads) // (1 << 30)
    return np.cumsum(np.array([max(1, weight // deviation) for weight in loads]))


def ranked(own_key, shape, amount, slope):
    listing = cumulative_ranks(amount, slope)
    lot = jax.random.randint(jax.random.fold_in(own_key, 1), shape, 0, int(listing[amount - 1]))
    rank = jnp.searchsorted(jnp.asarray(listing, jnp.int32), lot, side="right")
    return jax.random.permutation(jax.random.fold_in(own_key, 2), amount)[rank].astype(jnp.int32)


def scatter_about(own_key, shape, scale, most, split=(), kind=jnp.bfloat16):
    result = jax.random.normal(own_key, shape, jnp.float32) * scale
    if len(split) > 0:
        result = block_scale(own_key, shape, split, -0.22, 0.18) * result
    return jnp.clip(result, min=-most, max=most).astype(kind)


def setup_inputs(seed: int = 0) -> dict:
    keys = jax.random.split(jax.random.key(seed), 11)
    return {
        "ids": plant(ranked(keys[0], (RECS, FRAMES, NCB), VOCAB, 2), jax.random.fold_in(keys[0], 3), 0, VOCAB - 1).astype(jnp.int32),
        "tables": scatter_about(keys[1], (NCB, VOCAB, D), 0.35, 2.09375, ((1, 8), (2, 16))),
        "w_qkv": draw_w_qkv(jax.random.fold_in(keys[10], 71), 0),
        "w_out": scatter_about(keys[3], (D, D), D ** -0.5, 0.1875, ((0, 8),)),
        "attn_gain": jnp.clip(1.0 + 0.18 * jax.random.normal(keys[4], (D,), jnp.float32), 0.1, 1.9),
        "conv_gain": jnp.clip(1.0 + 0.18 * jax.random.normal(keys[5], (D,), jnp.float32), 0.1, 1.9),
        "conv_kernel": scatter_about(keys[6], (KT, D), KT ** -0.5, 1.0, (), jnp.float32),
        "back_list": draw_back_list(jax.random.fold_in(keys[10], 71), 0),
        "ahead_list": draw_ahead_list(jax.random.fold_in(keys[10], 71), 0),
        "cotangent": draw_cotangent(jax.random.fold_in(keys[10], 71), 0),
    }


EPSILON = 1e-06
NEGATIVE = -1e+30

def rounded(values):
    return lax.optimization_barrier(values.astype(jnp.bfloat16)).astype(jnp.float32)

def inverse_rms(features):
    return lax.rsqrt(lax.optimization_barrier(jnp.mean(features * features, axis=-1, keepdims=True)) + EPSILON)

def norm_back(features, inverse, gains, upstream):
    inner = lax.optimization_barrier(jnp.mean(features * gains * upstream, axis=-1, keepdims=True))
    return inverse * gains * upstream - features * inverse * inverse * inverse * inner

def silu_slope(conv_sum):
    sigmoid = jax.nn.sigmoid(conv_sum)
    return sigmoid * (1.0 + conv_sum * (1.0 - sigmoid))

def visible_flags(back_list, ahead_list):
    blocks = jnp.arange(BLOCKS, dtype=jnp.int32)
    columns = [jnp.ones((BLOCKS,), dtype=bool)]
    for step_back in range(WB):
        columns.append(jnp.any(back_list == (blocks - 1 - step_back)[:, None], axis=1))
    for step_ahead in range(WF):
        columns.append(jnp.any(ahead_list == (blocks + 1 + step_ahead)[:, None], axis=1))
    return jnp.stack(columns, axis=1)

def offset_list():
    return [0] + [-(step + 1) for step in range(WB)] + [step + 1 for step in range(WF)]

def shifted_blocks(tensor, offset):
    source = jnp.arange(BLOCKS, dtype=jnp.int32) + offset
    inside = (source >= 0) & (source < BLOCKS)
    picked = tensor[jnp.clip(source, 0, BLOCKS - 1)]
    inside = inside.reshape((BLOCKS,) + (1,) * (tensor.ndim - 1))
    return jnp.where(inside, picked, jnp.zeros_like(picked))

def block_probs(query_block, key_block, listed_block):
    scores = jnp.einsum('qhd,khd->hqk', query_block.astype(jnp.float32), key_block.astype(jnp.float32)) * HD ** (-0.5)
    visible = jnp.repeat(listed_block, BLOCK)
    scores = jnp.where(visible[None, None, :], scores, NEGATIVE)
    highest = lax.optimization_barrier(jnp.max(scores, axis=2, keepdims=True))
    weights = jnp.exp(scores - highest)
    return weights / lax.optimization_barrier(jnp.sum(weights, axis=2, keepdims=True))

def reference(ids, tables, w_qkv, w_out, attn_gain, conv_gain, conv_kernel, back_list, ahead_list, cotangent):
    listed = visible_flags(back_list, ahead_list)
    offsets = offset_list()
    rim_width = (KT - 1) // 2

    def recording(carry, inputs):
        token_ids, upstream_low = inputs
        summed = jnp.zeros((FRAMES, D), jnp.float32)
        for codebook in range(NCB):
            summed = summed + tables[codebook][token_ids[:, codebook]].astype(jnp.float32)
        embedded = summed.astype(jnp.bfloat16)
        features = embedded.astype(jnp.float32)
        attn_inverse = inverse_rms(features)
        normed = (features * attn_inverse * attn_gain).astype(jnp.bfloat16)
        projected = jnp.dot(normed, w_qkv, preferred_element_type=jnp.float32).astype(jnp.bfloat16)
        parts = projected.reshape(BLOCKS, BLOCK, 3, HEADS, HD)
        queries = parts[:, :, 0]
        key_rows = jnp.stack([shifted_blocks(parts[:, :, 1], offset) for offset in offsets], axis=1).reshape(BLOCKS, -1, HEADS, HD)
        value_rows = jnp.stack([shifted_blocks(parts[:, :, 2], offset) for offset in offsets], axis=1).reshape(BLOCKS, -1, HEADS, HD)

        def forward_block(items):
            query_block, key_block, value_block, listed_block = items
            probs_low = rounded(block_probs(query_block, key_block, listed_block))
            return jnp.einsum('hqk,khd->qhd', probs_low, value_block.astype(jnp.float32)).astype(jnp.bfloat16)
        mixed = lax.map(forward_block, (queries, key_rows, value_rows, listed)).reshape(FRAMES, D)
        projection = jnp.dot(mixed, w_out, preferred_element_type=jnp.float32)
        middle = (features + projection).astype(jnp.bfloat16)
        middle_wide = middle.astype(jnp.float32)
        conv_inverse = inverse_rms(middle_wide)
        conv_input = (middle_wide * conv_inverse * conv_gain).astype(jnp.bfloat16)
        padded = jnp.pad(conv_input.astype(jnp.float32), ((rim_width, rim_width), (0, 0)))
        conv_sum = jnp.zeros((FRAMES, D), jnp.float32)
        for tap_index in range(KT):
            conv_sum = conv_sum + conv_kernel[tap_index] * padded[tap_index:tap_index + FRAMES]
        block_out = (middle_wide + jax.nn.silu(conv_sum)).astype(jnp.bfloat16)
        upstream = upstream_low.astype(jnp.float32)
        grad_conv = rounded(upstream * silu_slope(conv_sum))
        grad_padded = jnp.pad(grad_conv, ((rim_width, rim_width), (0, 0)))
        kernel_rows = []
        grad_input = jnp.zeros((FRAMES, D), jnp.float32)
        for tap_index in range(KT):
            kernel_rows.append(lax.optimization_barrier(jnp.sum(grad_conv * padded[tap_index:tap_index + FRAMES], axis=0)))
            start_row = 2 * rim_width - tap_index
            grad_input = grad_input + conv_kernel[tap_index] * grad_padded[start_row:start_row + FRAMES]
        grad_middle = (upstream + norm_back(middle_wide, conv_inverse, conv_gain, grad_input)).astype(jnp.bfloat16)
        grad_mixed = jnp.dot(grad_middle, w_out.T, preferred_element_type=jnp.float32).astype(jnp.bfloat16)
        grad_wout = jnp.dot(mixed.T, grad_middle, preferred_element_type=jnp.float32)

        def backward_block(items):
            query_block, key_block, value_block, listed_block, grad_block = items
            probs = block_probs(query_block, key_block, listed_block)
            probs_low = rounded(probs)
            grad_wide = grad_block.astype(jnp.float32)
            grad_probs = jnp.einsum('qhd,khd->hqk', grad_wide, value_block.astype(jnp.float32))
            row_sum = lax.optimization_barrier(jnp.sum(probs * grad_probs, axis=2, keepdims=True))
            grad_scores = rounded(probs * (grad_probs - row_sum) * HD ** (-0.5))
            grad_query = jnp.einsum('hqk,khd->qhd', grad_scores, key_block.astype(jnp.float32))
            grad_key = jnp.einsum('hqk,qhd->khd', grad_scores, query_block.astype(jnp.float32))
            grad_value = jnp.einsum('hqk,qhd->khd', probs_low, grad_wide)
            return (grad_query, grad_key, grad_value)
        grad_query, grad_key, grad_value = lax.map(backward_block, (queries, key_rows, value_rows, listed, grad_mixed.reshape(BLOCKS, BLOCK, HEADS, HD)))
        seen_count = 1 + WB + WF
        pairs = jnp.concatenate([grad_key.reshape(BLOCKS, seen_count, BLOCK, D), grad_value.reshape(BLOCKS, seen_count, BLOCK, D)], axis=3)
        total = pairs[:, 0]
        for position in range(1, seen_count):
            total = total + shifted_blocks(rounded(pairs[:, position]), -offsets[position])
        grad_projected = jnp.concatenate([grad_query.reshape(FRAMES, D).astype(jnp.bfloat16), total.reshape(FRAMES, 2 * D).astype(jnp.bfloat16)], axis=1)
        grad_wqkv = jnp.dot(normed.T, grad_projected, preferred_element_type=jnp.float32)
        grad_normed = jnp.dot(grad_projected, w_qkv.T, preferred_element_type=jnp.float32)
        grad_embedded = (grad_middle.astype(jnp.float32) + norm_back(features, attn_inverse, attn_gain, grad_normed)).astype(jnp.bfloat16)
        carry = (carry[0] + grad_wqkv, carry[1] + grad_wout, carry[2] + jnp.stack(kernel_rows))
        return (carry, (block_out, grad_embedded))
    start = (jnp.zeros((D, 3 * D), jnp.float32), jnp.zeros((D, D), jnp.float32), jnp.zeros((KT, D), jnp.float32))
    totals, outputs = lax.scan(recording, start, (ids, cotangent))
    return (outputs[0], outputs[1], totals[0], totals[1], totals[2])
```

```python
import jax
import jax.numpy as jnp
from jax import lax
from jax.sharding import PartitionSpec as P

HEADS = 16


EPSILON = 1e-06
NEGATIVE = -1e30


def from_behind(value, axis, steps):
    count = lax.axis_size(axis)
    first, last = (max(0, -steps), min(count, count - steps))
    return lax.ppermute(value, axis, [(source, source + steps) for source in range(first, last)])


def with_halo(block, sides, width):
    for axis, dim in sides:
        count = lax.axis_size(axis)
        forward = [(i, i + 1) for i in range(count - 1)]
        backward = [(target, source) for source, target in forward]
        low = lax.ppermute(
            lax.slice_in_dim(block, block.shape[dim] - width, None, axis=dim), axis, forward
        )
        high = lax.ppermute(lax.slice_in_dim(block, 0, width, axis=dim), axis, backward)
        block = jnp.concatenate([low, block, high], axis=dim)
    return block


def inverse_rms(features):
    return lax.rsqrt(jnp.mean(features * features, axis=-1, keepdims=True) + EPSILON)


def norm_back(features, inverse, gains, upstream):
    inner = jnp.mean(features * gains * upstream, axis=-1, keepdims=True)
    return inverse * gains * upstream - features * inverse * inverse * inverse * inner


def silu_slope(conv_sum):
    sigmoid = jax.nn.sigmoid(conv_sum)
    return sigmoid * (1.0 + conv_sum * (1.0 - sigmoid))


def block_scores(queries, key_block, listed_block, score_scale):
    return jnp.where(
        listed_block,
        jnp.einsum("rqhd,rkhd->rhqk", queries, key_block, preferred_element_type=jnp.float32)
        * score_scale,
        NEGATIVE,
    )


def probabilities(queries, key_part, listed, score_scale):
    pieces = [
        block_scores(queries, key_part[:, position], listed[position], score_scale)
        for position in range(key_part.shape[1])
    ]
    scores = jnp.concatenate(pieces, axis=3)
    highest = jnp.max(scores, axis=3, keepdims=True)
    weights = jnp.exp(scores - highest)
    return weights / jnp.sum(weights, axis=3, keepdims=True)


def on_device(
    ids, tables, w_qkv, w_out, attn_gain, conv_gain, conv_kernel, back_list, ahead_list, cotangent
):
    recordings = ids.shape[0]
    frames_dev = ids.shape[1]
    head_count = HEADS
    tap_count = conv_kernel.shape[0]
    rim_width = (tap_count - 1) // 2
    group_width = 4
    group_count = head_count // group_width
    ids_whole = lax.all_gather(ids, "ctx", axis=1, tiled=True)
    table_whole = lax.all_gather(tables, "dp", axis=1, tiled=True)
    columns = jnp.zeros(ids_whole.shape[:2] + (table_whole.shape[2],), jnp.float32)
    for codebook in range(table_whole.shape[0]):
        columns = columns + jnp.take(
            table_whole[codebook], ids_whole[:, :, codebook], axis=0
        ).astype(jnp.float32)
    embedded = lax.all_to_all(
        columns.astype(jnp.bfloat16), "ctx", split_axis=1, concat_axis=2, tiled=True
    )
    weight_qkv, weight_out = (
        lax.all_gather(w_qkv, "dp", axis=0, tiled=True),
        lax.all_gather(w_out, "dp", axis=0, tiled=True),
    )
    model_width = weight_out.shape[0]
    head_size = model_width // head_count
    score_scale = head_size ** (-0.5)
    features = embedded.astype(jnp.float32).reshape(-1, model_width)
    attn_inverse = inverse_rms(features)
    normed = (features * attn_inverse * attn_gain).astype(jnp.bfloat16)
    projected = jnp.dot(normed, weight_qkv, preferred_element_type=jnp.float32).astype(jnp.bfloat16)
    projected = projected.reshape(recordings, frames_dev, 3 * model_width)
    own_pairs = projected[:, :, model_width:]
    ctx_index = lax.axis_index("ctx")
    back_row = lax.dynamic_index_in_dim(back_list, ctx_index, 0, keepdims=False)
    ahead_row = lax.dynamic_index_in_dim(ahead_list, ctx_index, 0, keepdims=False)
    offsets = [-(step + 1) for step in range(back_list.shape[1])] + [1]
    listed_items = [jnp.array(True)]
    pair_blocks = [own_pairs]
    for offset in offsets:
        list_row = back_row if offset < 0 else ahead_row
        listed_items.append(jnp.any(list_row == ctx_index + offset))
        pair_blocks.append(from_behind(own_pairs, "ctx", -offset))
    listed = jnp.stack(listed_items)
    seen_count = len(pair_blocks)
    stacked = jnp.stack(pair_blocks, axis=1)
    key_all = stacked[..., :model_width].reshape(
        recordings, seen_count, frames_dev, head_count, head_size
    )
    value_all = stacked[..., model_width:].reshape(
        recordings, seen_count, frames_dev, head_count, head_size
    )
    query_all = projected[:, :, :model_width].reshape(recordings, frames_dev, head_count, head_size)

    def forward_group(group):
        first_head = group * group_width
        queries = lax.dynamic_slice_in_dim(query_all, first_head, group_width, 2)
        key_part = lax.dynamic_slice_in_dim(key_all, first_head, group_width, 3)
        value_part = lax.dynamic_slice_in_dim(value_all, first_head, group_width, 3)
        probs_low = probabilities(queries, key_part, listed, score_scale).astype(jnp.bfloat16)
        value_flat = value_part.reshape(recordings, -1, group_width, head_size)
        return jnp.einsum(
            "rhqk,rkhd->rqhd", probs_low, value_flat, preferred_element_type=jnp.float32
        ).astype(jnp.bfloat16)

    mixed = lax.map(forward_group, jnp.arange(group_count, dtype=jnp.int32))
    mixed = jnp.moveaxis(mixed, 0, 2).reshape(recordings * frames_dev, model_width)
    projection = jnp.dot(mixed, weight_out, preferred_element_type=jnp.float32)
    middle = (features + projection).astype(jnp.bfloat16)
    middle_wide = middle.astype(jnp.float32)
    conv_inverse = inverse_rms(middle_wide)
    conv_input = (
        (middle_wide * conv_inverse * conv_gain)
        .astype(jnp.bfloat16)
        .reshape(recordings, frames_dev, model_width)
    )
    padded = with_halo(conv_input, (("ctx", 1),), rim_width).astype(jnp.float32)

    conv_sum = jnp.zeros((recordings, frames_dev, model_width), jnp.float32)
    for tap_index in range(tap_count):
        conv_sum = conv_sum + conv_kernel[tap_index] * padded[:, tap_index : tap_index + frames_dev]
    middle_frames = middle_wide.reshape(recordings, frames_dev, model_width)
    block_out = (middle_frames + jax.nn.silu(conv_sum)).astype(jnp.bfloat16)
    upstream = cotangent.astype(jnp.float32)
    grad_conv_low = (upstream * silu_slope(conv_sum)).astype(jnp.bfloat16)
    grad_conv = lax.optimization_barrier(grad_conv_low).astype(jnp.float32)
    grad_padded = with_halo(grad_conv_low, (("ctx", 1),), rim_width).astype(jnp.float32)

    grad_input = jnp.zeros((recordings, frames_dev, model_width), jnp.float32)
    kernel_list = []
    for tap_index in range(tap_count):
        window = padded[:, tap_index : tap_index + frames_dev]
        kernel_list.append(jnp.sum(grad_conv * window, axis=(0, 1)))
        start_row = 2 * rim_width - tap_index
        grad_input = grad_input + conv_kernel[tap_index] * grad_padded[
            :, start_row : start_row + frames_dev
        ]
    kernel_rows = jnp.stack(kernel_list)
    kernel_dp = lax.psum(kernel_rows, "dp")
    grad_middle = (
        upstream.reshape(-1, model_width)
        + norm_back(middle_wide, conv_inverse, conv_gain, grad_input.reshape(-1, model_width))
    ).astype(jnp.bfloat16)
    contract_rows = (((0,), (0,)), ((), ()))
    contract_columns = (((1,), (1,)), ((), ()))
    grad_mixed = lax.dot_general(
        grad_middle, weight_out, contract_columns, preferred_element_type=jnp.float32
    ).astype(jnp.bfloat16)
    mixed_columns = lax.all_to_all(mixed, "dp", split_axis=1, concat_axis=0, tiled=True)
    middle_rows = lax.all_gather(grad_middle, "dp", axis=0, tiled=True)
    grad_wout = lax.dot_general(
        mixed_columns, middle_rows, contract_rows, preferred_element_type=jnp.float32
    )
    grad_heads = grad_mixed.reshape(recordings, frames_dev, head_count, head_size)

    def backward_group(group):
        first_head = group * group_width
        queries = lax.dynamic_slice_in_dim(query_all, first_head, group_width, 2)
        key_part = lax.dynamic_slice_in_dim(key_all, first_head, group_width, 3)
        value_part = lax.dynamic_slice_in_dim(value_all, first_head, group_width, 3)
        grad_part = lax.dynamic_slice_in_dim(grad_heads, first_head, group_width, 2)
        probs = probabilities(queries, key_part, listed, score_scale)
        probs_low = probs.astype(jnp.bfloat16)
        key_flat = key_part.reshape(recordings, -1, group_width, head_size)
        value_flat = value_part.reshape(recordings, -1, group_width, head_size)
        grad_probs = jnp.einsum(
            "rqhd,rkhd->rhqk", grad_part, value_flat, preferred_element_type=jnp.float32
        )
        row_sum = jnp.sum(probs * grad_probs, axis=3, keepdims=True)
        grad_scores = (probs * (grad_probs - row_sum) * score_scale).astype(jnp.bfloat16)
        grad_query = jnp.einsum(
            "rhqk,rkhd->rqhd", grad_scores, key_flat, preferred_element_type=jnp.float32
        )
        grad_key = jnp.einsum(
            "rhqk,rqhd->rkhd", grad_scores, queries, preferred_element_type=jnp.float32
        )
        grad_value = jnp.einsum(
            "rhqk,rqhd->rkhd", probs_low, grad_part, preferred_element_type=jnp.float32
        )
        return (grad_query, grad_key, grad_value)

    grad_query, grad_key, grad_value = lax.map(
        backward_group, jnp.arange(group_count, dtype=jnp.int32)
    )
    grad_query = jnp.moveaxis(grad_query, 0, 2).reshape(recordings * frames_dev, model_width)
    grad_key = jnp.moveaxis(grad_key, 0, 2).reshape(recordings, seen_count, frames_dev, model_width)
    grad_value = jnp.moveaxis(grad_value, 0, 2).reshape(
        recordings, seen_count, frames_dev, model_width
    )
    pair_total = jnp.concatenate([grad_key[:, 0], grad_value[:, 0]], axis=2)
    for position, offset in enumerate(offsets):
        outgoing = jnp.concatenate(
            [grad_key[:, position + 1], grad_value[:, position + 1]], axis=2
        ).astype(jnp.bfloat16)
        arrived = from_behind(outgoing, "ctx", offset)
        pair_total = pair_total + arrived.astype(jnp.float32)
    grad_projected = jnp.concatenate(
        [
            grad_query.astype(jnp.bfloat16),
            pair_total.reshape(recordings * frames_dev, 2 * model_width).astype(jnp.bfloat16),
        ],
        axis=1,
    )
    normed_columns = lax.all_to_all(normed, "dp", split_axis=1, concat_axis=0, tiled=True)
    projected_rows = lax.all_gather(grad_projected, "dp", axis=0, tiled=True)
    grad_wqkv = lax.dot_general(
        normed_columns, projected_rows, contract_rows, preferred_element_type=jnp.float32
    )
    grad_normed = lax.dot_general(
        grad_projected, weight_qkv, contract_columns, preferred_element_type=jnp.float32
    )
    grad_embedded = (
        grad_middle.astype(jnp.float32) + norm_back(features, attn_inverse, attn_gain, grad_normed)
    ).astype(jnp.bfloat16)
    row_width = grad_wqkv.shape[1] + grad_wout.shape[1]
    kernel_padded = jnp.pad(kernel_dp, ((0, (-tap_count * model_width) % row_width // model_width), (0, 0)))
    kernel_packed = kernel_padded.reshape(-1, row_width)
    packed = jnp.concatenate(
        [jnp.concatenate([grad_wqkv, grad_wout], axis=1), kernel_packed], axis=0
    )
    summed = lax.psum(packed, "ctx")
    shard_rows = grad_wqkv.shape[0]
    grad_qkv = summed[:shard_rows, : grad_wqkv.shape[1]]
    grad_out = summed[:shard_rows, grad_wqkv.shape[1] :]
    grad_kernel = summed[shard_rows:].reshape(-1, model_width)[:tap_count]
    return (
        block_out,
        grad_embedded.reshape(recordings, frames_dev, model_width),
        grad_qkv,
        grad_out,
        grad_kernel,
    )


def solution(mesh):
    in_specs = (
        P("dp", "ctx", None),
        P(None, "dp", "ctx"),
        P("dp", None),
        P("dp", None),
        P(),
        P(),
        P(),
        P(),
        P(),
        P("dp", "ctx", None),
    )
    out_specs = (P("dp", "ctx", None), P("dp", "ctx", None), P("dp", None), P("dp", None), P())
    return jax.shard_map(
        on_device, mesh=mesh, in_specs=in_specs, out_specs=out_specs, check_vma=False
    )
```

```python
import jax
import jax.numpy as jnp
from jax import lax
from jax.sharding import PartitionSpec as P

HEADS = 16


EPSILON = 1e-06
NEGATIVE = -1e30


def from_behind(value, axis, steps):
    count = lax.axis_size(axis)
    first, last = (max(0, -steps), min(count, count - steps))
    return lax.ppermute(value, axis, [(source, source + steps) for source in range(first, last)])


def with_halo(block, sides, width):
    for axis, dim in sides:
        count = lax.axis_size(axis)
        forward = [(i, i + 1) for i in range(count - 1)]
        backward = [(target, source) for source, target in forward]
        low = lax.ppermute(
            lax.slice_in_dim(block, block.shape[dim] - width, None, axis=dim), axis, forward
        )
        high = lax.ppermute(lax.slice_in_dim(block, 0, width, axis=dim), axis, backward)
        block = jnp.concatenate([low, block, high], axis=dim)
    return block


def inverse_rms(features):
    return lax.rsqrt(jnp.mean(features * features, axis=-1, keepdims=True) + EPSILON)


def norm_back(features, inverse, gains, upstream):
    inner = jnp.mean(features * gains * upstream, axis=-1, keepdims=True)
    return inverse * gains * upstream - features * inverse * inverse * inverse * inner


def silu_slope(conv_sum):
    sigmoid = jax.nn.sigmoid(conv_sum)
    return sigmoid * (1.0 + conv_sum * (1.0 - sigmoid))


def block_scores(queries, key_block, listed_block, score_scale):
    return jnp.where(
        listed_block,
        jnp.einsum("rqhd,rkhd->rhqk", queries, key_block, preferred_element_type=jnp.float32)
        * score_scale,
        NEGATIVE,
    )


def probabilities(queries, key_part, listed, score_scale):
    pieces = [
        block_scores(queries, key_part[:, position], listed[position], score_scale)
        for position in range(key_part.shape[1])
    ]
    scores = jnp.concatenate(pieces, axis=3)
    highest = jnp.max(scores, axis=3, keepdims=True)
    weights = jnp.exp(scores - highest)
    return weights / jnp.sum(weights, axis=3, keepdims=True)


def on_device(
    ids, tables, w_qkv, w_out, attn_gain, conv_gain, conv_kernel, back_list, ahead_list, cotangent
):
    recordings = ids.shape[0]
    frames_dev = ids.shape[1]
    head_count = HEADS
    tap_count = conv_kernel.shape[0]
    rim_width = (tap_count - 1) // 2
    group_width = 4
    group_count = head_count // group_width
    ids_whole = lax.all_gather(ids, "ctx", axis=1, tiled=True)
    table_whole = lax.all_gather(tables, "dp", axis=1, tiled=True)
    vocab = table_whole.shape[1]
    entries = lax.broadcasted_iota(jnp.int32, (1, vocab), 1)
    columns = jnp.zeros((ids_whole.shape[1], table_whole.shape[2]), jnp.float32)
    for codebook in range(table_whole.shape[0]):
        picks = (ids_whole[0, :, codebook][:, None] == entries).astype(jnp.bfloat16)
        columns = columns + jnp.dot(
            picks, table_whole[codebook], preferred_element_type=jnp.float32
        )
    columns = columns[None]
    embedded = lax.all_to_all(
        columns.astype(jnp.bfloat16), "ctx", split_axis=1, concat_axis=2, tiled=True
    )
    weight_qkv, weight_out = (
        lax.all_gather(w_qkv, "dp", axis=0, tiled=True),
        lax.all_gather(w_out, "dp", axis=0, tiled=True),
    )
    model_width = weight_out.shape[0]
    head_size = model_width // head_count
    score_scale = head_size ** (-0.5)
    features = embedded.astype(jnp.float32).reshape(-1, model_width)
    attn_inverse = inverse_rms(features)
    normed = (features * attn_inverse * attn_gain).astype(jnp.bfloat16)
    projected = jnp.dot(normed, weight_qkv, preferred_element_type=jnp.float32).astype(jnp.bfloat16)
    projected = projected.reshape(recordings, frames_dev, 3 * model_width)
    own_pairs = projected[:, :, model_width:]
    ctx_index = lax.axis_index("ctx")
    back_row = lax.dynamic_index_in_dim(back_list, ctx_index, 0, keepdims=False)
    ahead_row = lax.dynamic_index_in_dim(ahead_list, ctx_index, 0, keepdims=False)
    offsets = [-(step + 1) for step in range(back_list.shape[1])] + [1]
    listed_items = [jnp.array(True)]
    pair_blocks = [own_pairs]
    for offset in offsets:
        list_row = back_row if offset < 0 else ahead_row
        listed_items.append(jnp.any(list_row == ctx_index + offset))
        pair_blocks.append(from_behind(own_pairs, "ctx", -offset))
    listed = jnp.stack(listed_items)
    seen_count = len(pair_blocks)
    stacked = jnp.stack(pair_blocks, axis=1)
    key_all = stacked[..., :model_width].reshape(
        recordings, seen_count, frames_dev, head_count, head_size
    )
    value_all = stacked[..., model_width:].reshape(
        recordings, seen_count, frames_dev, head_count, head_size
    )
    query_all = projected[:, :, :model_width].reshape(recordings, frames_dev, head_count, head_size)

    def forward_group(group):
        first_head = group * group_width
        queries = lax.dynamic_slice_in_dim(query_all, first_head, group_width, 2)
        key_part = lax.dynamic_slice_in_dim(key_all, first_head, group_width, 3)
        value_part = lax.dynamic_slice_in_dim(value_all, first_head, group_width, 3)
        probs_low = probabilities(queries, key_part, listed, score_scale).astype(jnp.bfloat16)
        value_flat = value_part.reshape(recordings, -1, group_width, head_size)
        return jnp.einsum(
            "rhqk,rkhd->rqhd", probs_low, value_flat, preferred_element_type=jnp.float32
        ).astype(jnp.bfloat16)

    mixed = lax.map(forward_group, jnp.arange(group_count, dtype=jnp.int32))
    mixed = jnp.moveaxis(mixed, 0, 2).reshape(recordings * frames_dev, model_width)
    projection = jnp.dot(mixed, weight_out, preferred_element_type=jnp.float32)
    middle = (features + projection).astype(jnp.bfloat16)
    middle_wide = middle.astype(jnp.float32)
    conv_inverse = inverse_rms(middle_wide)
    conv_input = (
        (middle_wide * conv_inverse * conv_gain)
        .astype(jnp.bfloat16)
        .reshape(recordings, frames_dev, model_width)
    )
    padded = with_halo(conv_input, (("ctx", 1),), rim_width).astype(jnp.float32)

    conv_sum = jnp.zeros((recordings, frames_dev, model_width), jnp.float32)
    for tap_index in range(tap_count):
        conv_sum = conv_sum + conv_kernel[tap_index] * padded[:, tap_index : tap_index + frames_dev]
    middle_frames = middle_wide.reshape(recordings, frames_dev, model_width)
    block_out = (middle_frames + jax.nn.silu(conv_sum)).astype(jnp.bfloat16)
    upstream = cotangent.astype(jnp.float32)
    grad_conv_low = (upstream * silu_slope(conv_sum)).astype(jnp.bfloat16)
    grad_conv = lax.optimization_barrier(grad_conv_low).astype(jnp.float32)
    grad_padded = with_halo(grad_conv_low, (("ctx", 1),), rim_width).astype(jnp.float32)

    grad_input = jnp.zeros((recordings, frames_dev, model_width), jnp.float32)
    kernel_list = []
    for tap_index in range(tap_count):
        window = padded[:, tap_index : tap_index + frames_dev]
        kernel_list.append(jnp.sum(grad_conv * window, axis=(0, 1)))
        start_row = 2 * rim_width - tap_index
        grad_input = grad_input + conv_kernel[tap_index] * grad_padded[
            :, start_row : start_row + frames_dev
        ]
    kernel_rows = jnp.stack(kernel_list)
    kernel_dp = lax.psum(kernel_rows, "dp")
    grad_middle = (
        upstream.reshape(-1, model_width)
        + norm_back(middle_wide, conv_inverse, conv_gain, grad_input.reshape(-1, model_width))
    ).astype(jnp.bfloat16)
    contract_rows = (((0,), (0,)), ((), ()))
    contract_columns = (((1,), (1,)), ((), ()))
    grad_mixed = lax.dot_general(
        grad_middle, weight_out, contract_columns, preferred_element_type=jnp.float32
    ).astype(jnp.bfloat16)
    dp_index = lax.axis_index("dp")
    shard_width = model_width // lax.axis_size("dp")
    mixed_columns = lax.dynamic_slice_in_dim(
        lax.all_gather(mixed, "dp", axis=0, tiled=True), dp_index * shard_width, shard_width, 1
    )
    middle_rows = lax.all_gather(grad_middle, "dp", axis=0, tiled=True)
    grad_wout = lax.dot_general(
        mixed_columns, middle_rows, contract_rows, preferred_element_type=jnp.float32
    )
    grad_heads = grad_mixed.reshape(recordings, frames_dev, head_count, head_size)

    def backward_group(group):
        first_head = group * group_width
        queries = lax.dynamic_slice_in_dim(query_all, first_head, group_width, 2)
        key_part = lax.dynamic_slice_in_dim(key_all, first_head, group_width, 3)
        value_part = lax.dynamic_slice_in_dim(value_all, first_head, group_width, 3)
        grad_part = lax.dynamic_slice_in_dim(grad_heads, first_head, group_width, 2)
        probs = probabilities(queries, key_part, listed, score_scale)
        probs_low = probs.astype(jnp.bfloat16)
        key_flat = key_part.reshape(recordings, -1, group_width, head_size)
        value_flat = value_part.reshape(recordings, -1, group_width, head_size)
        grad_probs = jnp.einsum(
            "rqhd,rkhd->rhqk", grad_part, value_flat, preferred_element_type=jnp.float32
        )
        row_sum = jnp.sum(probs * grad_probs, axis=3, keepdims=True)
        grad_scores = (probs * (grad_probs - row_sum) * score_scale).astype(jnp.bfloat16)
        grad_query = jnp.einsum(
            "rhqk,rkhd->rqhd", grad_scores, key_flat, preferred_element_type=jnp.float32
        )
        grad_key = jnp.einsum(
            "rhqk,rqhd->rkhd", grad_scores, queries, preferred_element_type=jnp.float32
        )
        grad_value = jnp.einsum(
            "rhqk,rqhd->rkhd", probs_low, grad_part, preferred_element_type=jnp.float32
        )
        return (grad_query, grad_key, grad_value)

    grad_query, grad_key, grad_value = lax.map(
        backward_group, jnp.arange(group_count, dtype=jnp.int32)
    )
    grad_query = jnp.moveaxis(grad_query, 0, 2).reshape(recordings * frames_dev, model_width)
    grad_key = jnp.moveaxis(grad_key, 0, 2).reshape(recordings, seen_count, frames_dev, model_width)
    grad_value = jnp.moveaxis(grad_value, 0, 2).reshape(
        recordings, seen_count, frames_dev, model_width
    )
    pair_total = jnp.concatenate([grad_key[:, 0], grad_value[:, 0]], axis=2)
    for position, offset in enumerate(offsets):
        outgoing = jnp.concatenate(
            [grad_key[:, position + 1], grad_value[:, position + 1]], axis=2
        ).astype(jnp.bfloat16)
        arrived = from_behind(outgoing, "ctx", offset)
        pair_total = pair_total + arrived.astype(jnp.float32)
    grad_projected = jnp.concatenate(
        [
            grad_query.astype(jnp.bfloat16),
            pair_total.reshape(recordings * frames_dev, 2 * model_width).astype(jnp.bfloat16),
        ],
        axis=1,
    )
    normed_columns = lax.dynamic_slice_in_dim(
        lax.all_gather(normed, "dp", axis=0, tiled=True), dp_index * shard_width, shard_width, 1
    )
    query_rows = lax.all_gather(grad_projected[:, :model_width], "dp", axis=0, tiled=True)
    grad_wq = lax.dot_general(
        normed_columns, query_rows, contract_rows, preferred_element_type=jnp.float32
    )
    early = lax.psum(jnp.concatenate([grad_wq, grad_wout], axis=1), "ctx")
    early, pair_part = lax.optimization_barrier((early, grad_projected[:, model_width:]))
    pair_rows = lax.all_gather(pair_part, "dp", axis=0, tiled=True)
    grad_wkv = lax.dot_general(
        normed_columns, pair_rows, contract_rows, preferred_element_type=jnp.float32
    )
    grad_normed = lax.dot_general(
        grad_projected, weight_qkv, contract_columns, preferred_element_type=jnp.float32
    )
    grad_embedded = (
        grad_middle.astype(jnp.float32) + norm_back(features, attn_inverse, attn_gain, grad_normed)
    ).astype(jnp.bfloat16)
    row_width = grad_wkv.shape[1]
    kernel_padded = jnp.pad(
        kernel_dp, ((0, (-tap_count * model_width) % row_width // model_width), (0, 0))
    )
    late = lax.psum(
        jnp.concatenate([grad_wkv, kernel_padded.reshape(-1, row_width)], axis=0), "ctx"
    )
    shard_rows = grad_wkv.shape[0]
    grad_qkv = jnp.concatenate(
        [early[:, :model_width], late[:shard_rows]], axis=1
    )
    grad_out = early[:, model_width:]
    grad_kernel = late[shard_rows:].reshape(-1, model_width)[:tap_count]
    return (
        block_out,
        grad_embedded.reshape(recordings, frames_dev, model_width),
        grad_qkv,
        grad_out,
        grad_kernel,
    )


def solution(mesh):
    in_specs = (
        P("dp", "ctx", None),
        P(None, "dp", "ctx"),
        P("dp", None),
        P("dp", None),
        P(),
        P(),
        P(),
        P(),
        P(),
        P("dp", "ctx", None),
    )
    out_specs = (P("dp", "ctx", None), P("dp", "ctx", None), P("dp", None), P("dp", None), P())
    return jax.shard_map(
        on_device, mesh=mesh, in_specs=in_specs, out_specs=out_specs, check_vma=False
    )
```

```python
import jax
import jax.numpy as jnp
from jax import lax
from jax.sharding import PartitionSpec as P

HEADS = 16


EPSILON = 1e-06
NEGATIVE = -1e30


def from_behind(value, axis, steps):
    count = lax.axis_size(axis)
    first, last = (max(0, -steps), min(count, count - steps))
    return lax.ppermute(value, axis, [(source, source + steps) for source in range(first, last)])


def with_halo(block, sides, width):
    for axis, dim in sides:
        count = lax.axis_size(axis)
        forward = [(i, i + 1) for i in range(count - 1)]
        backward = [(target, source) for source, target in forward]
        low = lax.ppermute(
            lax.slice_in_dim(block, block.shape[dim] - width, None, axis=dim), axis, forward
        )
        high = lax.ppermute(lax.slice_in_dim(block, 0, width, axis=dim), axis, backward)
        block = jnp.concatenate([low, block, high], axis=dim)
    return block


def inverse_rms(features):
    return lax.rsqrt(jnp.mean(features * features, axis=-1, keepdims=True) + EPSILON)


def norm_back(features, inverse, gains, upstream):
    inner = jnp.mean(features * gains * upstream, axis=-1, keepdims=True)
    return inverse * gains * upstream - features * inverse * inverse * inverse * inner


def silu_slope(conv_sum):
    sigmoid = jax.nn.sigmoid(conv_sum)
    return sigmoid * (1.0 + conv_sum * (1.0 - sigmoid))


def block_scores(queries, key_block, listed_block, score_scale):
    return jnp.where(
        listed_block,
        jnp.einsum("rqhd,rkhd->rhqk", queries, key_block, preferred_element_type=jnp.float32)
        * score_scale,
        NEGATIVE,
    )


def probabilities(queries, key_part, listed, score_scale):
    pieces = [
        block_scores(queries, key_part[:, position], listed[position], score_scale)
        for position in range(key_part.shape[1])
    ]
    scores = jnp.concatenate(pieces, axis=3)
    highest = jnp.max(scores, axis=3, keepdims=True)
    weights = jnp.exp(scores - highest)
    return weights / jnp.sum(weights, axis=3, keepdims=True)


def on_device(
    ids, tables, w_qkv, w_out, attn_gain, conv_gain, conv_kernel, back_list, ahead_list, cotangent
):
    recordings = ids.shape[0]
    frames_dev = ids.shape[1]
    head_count = HEADS
    tap_count = conv_kernel.shape[0]
    rim_width = (tap_count - 1) // 2
    group_width = 4
    group_count = head_count // group_width
    ids_whole = lax.all_gather(ids, "ctx", axis=1, tiled=True)
    table_whole = lax.all_gather(tables, "dp", axis=1, tiled=True)
    vocab = table_whole.shape[1]
    entries = lax.broadcasted_iota(jnp.int32, (vocab, 1), 0)
    transposed = jnp.zeros((table_whole.shape[2], ids_whole.shape[1]), jnp.float32)
    for codebook in range(table_whole.shape[0]):
        picks = (entries == ids_whole[0, :, codebook][None, :]).astype(jnp.bfloat16)
        transposed = transposed + lax.dot_general(
            table_whole[codebook], picks, (((0,), (0,)), ((), ())),
            preferred_element_type=jnp.float32,
        )
    ctx_count = lax.axis_size("ctx")
    transposed = transposed.astype(jnp.bfloat16).reshape(transposed.shape[0], ctx_count, frames_dev)
    gathered = lax.all_to_all(transposed, "ctx", split_axis=1, concat_axis=0, tiled=True)
    embedded = gathered.reshape(-1, frames_dev).T[None]
    weight_qkv, weight_out = (
        lax.all_gather(w_qkv, "dp", axis=0, tiled=True),
        lax.all_gather(w_out, "dp", axis=0, tiled=True),
    )
    model_width = weight_out.shape[0]
    head_size = model_width // head_count
    score_scale = head_size ** (-0.5)
    features = embedded.astype(jnp.float32).reshape(-1, model_width)
    attn_inverse = inverse_rms(features)
    normed = (features * attn_inverse * attn_gain).astype(jnp.bfloat16)
    projected = jnp.dot(normed, weight_qkv, preferred_element_type=jnp.float32).astype(jnp.bfloat16)
    projected = projected.reshape(recordings, frames_dev, 3 * model_width)
    own_pairs = projected[:, :, model_width:]
    ctx_index = lax.axis_index("ctx")
    back_row = lax.dynamic_index_in_dim(back_list, ctx_index, 0, keepdims=False)
    ahead_row = lax.dynamic_index_in_dim(ahead_list, ctx_index, 0, keepdims=False)
    offsets = [-(step + 1) for step in range(back_list.shape[1])] + [1]
    listed_items = [jnp.array(True)]
    pair_blocks = [own_pairs]
    for offset in offsets:
        list_row = back_row if offset < 0 else ahead_row
        listed_items.append(jnp.any(list_row == ctx_index + offset))
        pair_blocks.append(from_behind(own_pairs, "ctx", -offset))
    listed = jnp.stack(listed_items)
    seen_count = len(pair_blocks)
    stacked = jnp.stack(pair_blocks, axis=1)
    key_all = stacked[..., :model_width].reshape(
        recordings, seen_count, frames_dev, head_count, head_size
    )
    value_all = stacked[..., model_width:].reshape(
        recordings, seen_count, frames_dev, head_count, head_size
    )
    query_all = projected[:, :, :model_width].reshape(recordings, frames_dev, head_count, head_size)

    def forward_group(group):
        first_head = group * group_width
        queries = lax.dynamic_slice_in_dim(query_all, first_head, group_width, 2)
        key_part = lax.dynamic_slice_in_dim(key_all, first_head, group_width, 3)
        value_part = lax.dynamic_slice_in_dim(value_all, first_head, group_width, 3)
        probs_low = probabilities(queries, key_part, listed, score_scale).astype(jnp.bfloat16)
        value_flat = value_part.reshape(recordings, -1, group_width, head_size)
        return jnp.einsum(
            "rhqk,rkhd->rqhd", probs_low, value_flat, preferred_element_type=jnp.float32
        ).astype(jnp.bfloat16)

    mixed = lax.map(forward_group, jnp.arange(group_count, dtype=jnp.int32))
    mixed = jnp.moveaxis(mixed, 0, 2).reshape(recordings * frames_dev, model_width)
    projection = jnp.dot(mixed, weight_out, preferred_element_type=jnp.float32)
    middle = (features + projection).astype(jnp.bfloat16)
    middle_wide = middle.astype(jnp.float32)
    conv_inverse = inverse_rms(middle_wide)
    conv_input = (
        (middle_wide * conv_inverse * conv_gain)
        .astype(jnp.bfloat16)
        .reshape(recordings, frames_dev, model_width)
    )
    padded = with_halo(conv_input, (("ctx", 1),), rim_width).astype(jnp.float32)

    conv_sum = jnp.zeros((recordings, frames_dev, model_width), jnp.float32)
    for tap_index in range(tap_count):
        conv_sum = conv_sum + conv_kernel[tap_index] * padded[:, tap_index : tap_index + frames_dev]
    middle_frames = middle_wide.reshape(recordings, frames_dev, model_width)
    block_out = (middle_frames + jax.nn.silu(conv_sum)).astype(jnp.bfloat16)
    upstream = cotangent.astype(jnp.float32)
    grad_conv_low = (upstream * silu_slope(conv_sum)).astype(jnp.bfloat16)
    grad_conv = lax.optimization_barrier(grad_conv_low).astype(jnp.float32)
    grad_padded = with_halo(grad_conv_low, (("ctx", 1),), rim_width).astype(jnp.float32)

    grad_input = jnp.zeros((recordings, frames_dev, model_width), jnp.float32)
    kernel_list = []
    for tap_index in range(tap_count):
        window = padded[:, tap_index : tap_index + frames_dev]
        kernel_list.append(jnp.sum(grad_conv * window, axis=(0, 1)))
        start_row = 2 * rim_width - tap_index
        grad_input = grad_input + conv_kernel[tap_index] * grad_padded[
            :, start_row : start_row + frames_dev
        ]
    kernel_rows = jnp.stack(kernel_list)
    kernel_dp = jnp.sum(lax.all_gather(kernel_rows, "dp"), axis=0)
    grad_middle = (
        upstream.reshape(-1, model_width)
        + norm_back(middle_wide, conv_inverse, conv_gain, grad_input.reshape(-1, model_width))
    ).astype(jnp.bfloat16)
    contract_rows = (((0,), (0,)), ((), ()))
    contract_columns = (((1,), (1,)), ((), ()))
    grad_mixed = lax.dot_general(
        grad_middle, weight_out, contract_columns, preferred_element_type=jnp.float32
    ).astype(jnp.bfloat16)
    dp_index = lax.axis_index("dp")
    shard_width = model_width // lax.axis_size("dp")
    mixed_columns = lax.dynamic_slice_in_dim(
        lax.all_gather(mixed, "dp", axis=0, tiled=True), dp_index * shard_width, shard_width, 1
    )
    middle_rows = lax.all_gather(grad_middle, "dp", axis=0, tiled=True)
    grad_wout = lax.dot_general(
        mixed_columns, middle_rows, contract_rows, preferred_element_type=jnp.float32
    )
    grad_heads = grad_mixed.reshape(recordings, frames_dev, head_count, head_size)

    def backward_group(group):
        first_head = group * group_width
        queries = lax.dynamic_slice_in_dim(query_all, first_head, group_width, 2)
        key_part = lax.dynamic_slice_in_dim(key_all, first_head, group_width, 3)
        value_part = lax.dynamic_slice_in_dim(value_all, first_head, group_width, 3)
        grad_part = lax.dynamic_slice_in_dim(grad_heads, first_head, group_width, 2)
        probs = probabilities(queries, key_part, listed, score_scale)
        probs_low = probs.astype(jnp.bfloat16)
        key_flat = key_part.reshape(recordings, -1, group_width, head_size)
        value_flat = value_part.reshape(recordings, -1, group_width, head_size)
        grad_probs = jnp.einsum(
            "rqhd,rkhd->rhqk", grad_part, value_flat, preferred_element_type=jnp.float32
        )
        row_sum = jnp.sum(probs * grad_probs, axis=3, keepdims=True)
        grad_scores = (probs * (grad_probs - row_sum) * score_scale).astype(jnp.bfloat16)
        grad_query = jnp.einsum(
            "rhqk,rkhd->rqhd", grad_scores, key_flat, preferred_element_type=jnp.float32
        )
        grad_key = jnp.einsum(
            "rhqk,rqhd->rkhd", grad_scores, queries, preferred_element_type=jnp.float32
        )
        grad_value = jnp.einsum(
            "rhqk,rqhd->rkhd", probs_low, grad_part, preferred_element_type=jnp.float32
        )
        return (grad_query, grad_key, grad_value)

    grad_query, grad_key, grad_value = lax.map(
        backward_group, jnp.arange(group_count, dtype=jnp.int32)
    )
    kernel_dp, grad_query = lax.optimization_barrier((kernel_dp, grad_query))
    grad_query = jnp.moveaxis(grad_query, 0, 2).reshape(recordings * frames_dev, model_width)
    grad_key = jnp.moveaxis(grad_key, 0, 2).reshape(recordings, seen_count, frames_dev, model_width)
    grad_value = jnp.moveaxis(grad_value, 0, 2).reshape(
        recordings, seen_count, frames_dev, model_width
    )
    pair_total = jnp.concatenate([grad_key[:, 0], grad_value[:, 0]], axis=2)
    for position, offset in enumerate(offsets):
        outgoing = jnp.concatenate(
            [grad_key[:, position + 1], grad_value[:, position + 1]], axis=2
        ).astype(jnp.bfloat16)
        arrived = from_behind(outgoing, "ctx", offset)
        pair_total = pair_total + arrived.astype(jnp.float32)
    grad_projected = jnp.concatenate(
        [
            grad_query.astype(jnp.bfloat16),
            pair_total.reshape(recordings * frames_dev, 2 * model_width).astype(jnp.bfloat16),
        ],
        axis=1,
    )
    normed_columns = lax.dynamic_slice_in_dim(
        lax.all_gather(normed, "dp", axis=0, tiled=True), dp_index * shard_width, shard_width, 1
    )
    query_rows = lax.all_gather(grad_projected[:, :model_width], "dp", axis=0, tiled=True)
    grad_wq = lax.dot_general(
        normed_columns, query_rows, contract_rows, preferred_element_type=jnp.float32
    )
    pair_part = grad_projected[:, model_width:]
    pair_rows = lax.all_gather(pair_part, "dp", axis=0, tiled=True)
    grad_wkv = lax.dot_general(
        normed_columns, pair_rows, contract_rows, preferred_element_type=jnp.float32
    )
    grad_normed = lax.dot_general(
        grad_projected, weight_qkv, contract_columns, preferred_element_type=jnp.float32
    )
    grad_embedded = (
        grad_middle.astype(jnp.float32) + norm_back(features, attn_inverse, attn_gain, grad_normed)
    ).astype(jnp.bfloat16)
    weight_rows = jnp.concatenate([grad_wq, grad_wkv, grad_wout], axis=1)
    row_width = weight_rows.shape[1]
    kernel_padded = jnp.pad(
        kernel_dp, ((0, (-tap_count * model_width) % row_width // model_width), (0, 0))
    )
    summed = lax.psum(
        jnp.concatenate([weight_rows, kernel_padded.reshape(-1, row_width)], axis=0), "ctx"
    )
    shard_rows = weight_rows.shape[0]
    qkv_width = grad_wq.shape[1] + grad_wkv.shape[1]
    grad_qkv = summed[:shard_rows, :qkv_width]
    grad_out = summed[:shard_rows, qkv_width:]
    grad_kernel = summed[shard_rows:].reshape(-1, model_width)[:tap_count]
    return (
        block_out,
        grad_embedded.reshape(recordings, frames_dev, model_width),
        grad_qkv,
        grad_out,
        grad_kernel,
    )


def solution(mesh):
    in_specs = (
        P("dp", "ctx", None),
        P(None, "dp", "ctx"),
        P("dp", None),
        P("dp", None),
        P(),
        P(),
        P(),
        P(),
        P(),
        P("dp", "ctx", None),
    )
    out_specs = (P("dp", "ctx", None), P("dp", "ctx", None), P("dp", None), P("dp", None), P())
    return jax.shard_map(
        on_device, mesh=mesh, in_specs=in_specs, out_specs=out_specs, check_vma=False
    )
```

```python
import jax
import jax.numpy as jnp
from jax import lax
from jax.sharding import PartitionSpec as P

HEADS = 16


EPSILON = 1e-06
NEGATIVE = -1e30


def from_behind(value, axis, steps):
    count = lax.axis_size(axis)
    first, last = (max(0, -steps), min(count, count - steps))
    return lax.ppermute(value, axis, [(source, source + steps) for source in range(first, last)])


def with_halo(block, sides, width):
    for axis, dim in sides:
        count = lax.axis_size(axis)
        forward = [(i, i + 1) for i in range(count - 1)]
        backward = [(target, source) for source, target in forward]
        low = lax.ppermute(
            lax.slice_in_dim(block, block.shape[dim] - width, None, axis=dim), axis, forward
        )
        high = lax.ppermute(lax.slice_in_dim(block, 0, width, axis=dim), axis, backward)
        block = jnp.concatenate([low, block, high], axis=dim)
    return block


def inverse_rms(features):
    return lax.rsqrt(jnp.mean(features * features, axis=-1, keepdims=True) + EPSILON)


def norm_back(features, inverse, gains, upstream):
    inner = jnp.mean(features * gains * upstream, axis=-1, keepdims=True)
    return inverse * gains * upstream - features * inverse * inverse * inverse * inner


def silu_slope(conv_sum):
    sigmoid = jax.nn.sigmoid(conv_sum)
    return sigmoid * (1.0 + conv_sum * (1.0 - sigmoid))


def block_scores(queries, key_block, listed_block, score_scale):
    return jnp.where(
        listed_block,
        jnp.einsum("rqhd,rkhd->rhqk", queries, key_block, preferred_element_type=jnp.float32)
        * score_scale,
        NEGATIVE,
    )


def probabilities(queries, key_part, listed, score_scale):
    pieces = [
        block_scores(queries, key_part[:, position], listed[position], score_scale)
        for position in range(key_part.shape[1])
    ]
    scores = jnp.concatenate(pieces, axis=3)
    highest = jnp.max(scores, axis=3, keepdims=True)
    weights = jnp.exp(scores - highest)
    return weights / jnp.sum(weights, axis=3, keepdims=True)


def on_device(
    ids, tables, w_qkv, w_out, attn_gain, conv_gain, conv_kernel, back_list, ahead_list, cotangent
):
    recordings = ids.shape[0]
    frames_dev = ids.shape[1]
    head_count = HEADS
    tap_count = conv_kernel.shape[0]
    rim_width = (tap_count - 1) // 2
    ids_whole = lax.all_gather(ids, "ctx", axis=1, tiled=True)
    table_whole = lax.all_gather(tables, "dp", axis=1, tiled=True)
    vocab = table_whole.shape[1]
    entries = lax.broadcasted_iota(jnp.int32, (vocab, 1), 0)
    transposed = jnp.zeros((table_whole.shape[2], ids_whole.shape[1]), jnp.float32)
    for codebook in range(table_whole.shape[0]):
        picks = (entries == ids_whole[0, :, codebook][None, :]).astype(jnp.bfloat16)
        transposed = transposed + lax.dot_general(
            table_whole[codebook], picks, (((0,), (0,)), ((), ())),
            preferred_element_type=jnp.float32,
        )
    ctx_count = lax.axis_size("ctx")
    transposed = transposed.astype(jnp.bfloat16).reshape(transposed.shape[0], ctx_count, frames_dev)
    gathered = lax.all_to_all(transposed, "ctx", split_axis=1, concat_axis=0, tiled=True)
    embedded = gathered.reshape(-1, frames_dev).T[None]
    weight_qkv, weight_out = (
        lax.all_gather(w_qkv, "dp", axis=0, tiled=True),
        lax.all_gather(w_out, "dp", axis=0, tiled=True),
    )
    model_width = weight_out.shape[0]
    head_size = model_width // head_count
    score_scale = head_size ** (-0.5)
    features = embedded.astype(jnp.float32).reshape(-1, model_width)
    attn_inverse = inverse_rms(features)
    normed = (features * attn_inverse * attn_gain).astype(jnp.bfloat16)
    projected = jnp.dot(normed, weight_qkv, preferred_element_type=jnp.float32).astype(jnp.bfloat16)
    projected = projected.reshape(recordings, frames_dev, 3 * model_width)
    own_pairs = projected[:, :, model_width:]
    ctx_index = lax.axis_index("ctx")
    back_row = lax.dynamic_index_in_dim(back_list, ctx_index, 0, keepdims=False)
    ahead_row = lax.dynamic_index_in_dim(ahead_list, ctx_index, 0, keepdims=False)
    offsets = [-(step + 1) for step in range(back_list.shape[1])] + [1]
    listed_items = [jnp.array(True)]
    pair_blocks = [own_pairs]
    for offset in offsets:
        list_row = back_row if offset < 0 else ahead_row
        listed_items.append(jnp.any(list_row == ctx_index + offset))
        pair_blocks.append(from_behind(own_pairs, "ctx", -offset))
    listed = jnp.stack(listed_items)
    seen_count = len(pair_blocks)
    stacked = jnp.stack(pair_blocks, axis=1)
    key_all = stacked[..., :model_width].reshape(
        recordings, seen_count, frames_dev, head_count, head_size
    )
    value_all = stacked[..., model_width:].reshape(
        recordings, seen_count, frames_dev, head_count, head_size
    )
    query_all = projected[:, :, :model_width].reshape(recordings, frames_dev, head_count, head_size)

    key_flat = key_all.reshape(recordings, -1, head_count, head_size)
    value_flat = value_all.reshape(recordings, -1, head_count, head_size)
    visible = jnp.repeat(listed, frames_dev)
    scores = jnp.where(
        visible,
        jnp.einsum("rqhd,rkhd->rhqk", query_all, key_flat, preferred_element_type=jnp.float32)
        * score_scale,
        NEGATIVE,
    )
    highest = jnp.max(scores, axis=3, keepdims=True)
    weights = jnp.exp(scores - highest)
    probs = weights / jnp.sum(weights, axis=3, keepdims=True)
    probs_low = probs.astype(jnp.bfloat16)
    mixed = jnp.einsum(
        "rhqk,rkhd->rqhd", probs_low, value_flat, preferred_element_type=jnp.float32
    ).astype(jnp.bfloat16)
    mixed = mixed.reshape(recordings * frames_dev, model_width)
    projection = jnp.dot(mixed, weight_out, preferred_element_type=jnp.float32)
    middle = (features + projection).astype(jnp.bfloat16)
    middle_wide = middle.astype(jnp.float32)
    conv_inverse = inverse_rms(middle_wide)
    conv_input = (
        (middle_wide * conv_inverse * conv_gain)
        .astype(jnp.bfloat16)
        .reshape(recordings, frames_dev, model_width)
    )
    padded = with_halo(conv_input, (("ctx", 1),), rim_width).astype(jnp.float32)

    conv_sum = jnp.zeros((recordings, frames_dev, model_width), jnp.float32)
    for tap_index in range(tap_count):
        conv_sum = conv_sum + conv_kernel[tap_index] * padded[:, tap_index : tap_index + frames_dev]
    middle_frames = middle_wide.reshape(recordings, frames_dev, model_width)
    block_out = (middle_frames + jax.nn.silu(conv_sum)).astype(jnp.bfloat16)
    upstream = cotangent.astype(jnp.float32)
    grad_conv_low = (upstream * silu_slope(conv_sum)).astype(jnp.bfloat16)
    grad_conv = lax.optimization_barrier(grad_conv_low).astype(jnp.float32)
    grad_padded = with_halo(grad_conv_low, (("ctx", 1),), rim_width).astype(jnp.float32)

    grad_input = jnp.zeros((recordings, frames_dev, model_width), jnp.float32)
    kernel_list = []
    for tap_index in range(tap_count):
        window = padded[:, tap_index : tap_index + frames_dev]
        kernel_list.append(jnp.sum(grad_conv * window, axis=(0, 1)))
        start_row = 2 * rim_width - tap_index
        grad_input = grad_input + conv_kernel[tap_index] * grad_padded[
            :, start_row : start_row + frames_dev
        ]
    kernel_rows = jnp.stack(kernel_list)
    kernel_dp = jnp.sum(lax.all_gather(kernel_rows, "dp"), axis=0)
    grad_middle = (
        upstream.reshape(-1, model_width)
        + norm_back(middle_wide, conv_inverse, conv_gain, grad_input.reshape(-1, model_width))
    ).astype(jnp.bfloat16)
    contract_rows = (((0,), (0,)), ((), ()))
    contract_columns = (((1,), (1,)), ((), ()))
    grad_mixed = lax.dot_general(
        grad_middle, weight_out, contract_columns, preferred_element_type=jnp.float32
    ).astype(jnp.bfloat16)
    dp_index = lax.axis_index("dp")
    shard_width = model_width // lax.axis_size("dp")
    mixed_columns = lax.dynamic_slice_in_dim(
        lax.all_gather(mixed, "dp", axis=0, tiled=True), dp_index * shard_width, shard_width, 1
    )
    middle_rows = lax.all_gather(grad_middle, "dp", axis=0, tiled=True)
    grad_wout = lax.dot_general(
        mixed_columns, middle_rows, contract_rows, preferred_element_type=jnp.float32
    )
    grad_heads = grad_mixed.reshape(recordings, frames_dev, head_count, head_size)

    grad_probs = jnp.einsum(
        "rqhd,rkhd->rhqk", grad_heads, value_flat, preferred_element_type=jnp.float32
    )
    row_sum = jnp.sum(probs * grad_probs, axis=3, keepdims=True)
    grad_scores = (probs * (grad_probs - row_sum) * score_scale).astype(jnp.bfloat16)
    grad_query = jnp.einsum(
        "rhqk,rkhd->rqhd", grad_scores, key_flat, preferred_element_type=jnp.float32
    )
    grad_key = jnp.einsum(
        "rhqk,rqhd->rkhd", grad_scores, query_all, preferred_element_type=jnp.float32
    )
    grad_value = jnp.einsum(
        "rhqk,rqhd->rkhd", probs_low, grad_heads, preferred_element_type=jnp.float32
    )
    kernel_dp, grad_query = lax.optimization_barrier((kernel_dp, grad_query))
    grad_query = grad_query.reshape(recordings * frames_dev, model_width)
    grad_key = grad_key.reshape(recordings, seen_count, frames_dev, model_width)
    grad_value = grad_value.reshape(recordings, seen_count, frames_dev, model_width)
    pair_total = jnp.concatenate([grad_key[:, 0], grad_value[:, 0]], axis=2)
    for position, offset in enumerate(offsets):
        outgoing = jnp.concatenate(
            [grad_key[:, position + 1], grad_value[:, position + 1]], axis=2
        ).astype(jnp.bfloat16)
        arrived = from_behind(outgoing, "ctx", offset)
        pair_total = pair_total + arrived.astype(jnp.float32)
    grad_projected = jnp.concatenate(
        [
            grad_query.astype(jnp.bfloat16),
            pair_total.reshape(recordings * frames_dev, 2 * model_width).astype(jnp.bfloat16),
        ],
        axis=1,
    )
    normed_columns = lax.dynamic_slice_in_dim(
        lax.all_gather(normed, "dp", axis=0, tiled=True), dp_index * shard_width, shard_width, 1
    )
    query_rows = lax.all_gather(grad_projected[:, :model_width], "dp", axis=0, tiled=True)
    grad_wq = lax.dot_general(
        normed_columns, query_rows, contract_rows, preferred_element_type=jnp.float32
    )
    pair_part = grad_projected[:, model_width:]
    pair_rows = lax.all_gather(pair_part, "dp", axis=0, tiled=True)
    grad_wkv = lax.dot_general(
        normed_columns, pair_rows, contract_rows, preferred_element_type=jnp.float32
    )
    grad_normed = lax.dot_general(
        grad_projected, weight_qkv, contract_columns, preferred_element_type=jnp.float32
    )
    grad_embedded = (
        grad_middle.astype(jnp.float32) + norm_back(features, attn_inverse, attn_gain, grad_normed)
    ).astype(jnp.bfloat16)
    weight_rows = jnp.concatenate([grad_wq, grad_wkv, grad_wout], axis=1)
    row_width = weight_rows.shape[1]
    kernel_padded = jnp.pad(
        kernel_dp, ((0, (-tap_count * model_width) % row_width // model_width), (0, 0))
    )
    summed = lax.psum(
        jnp.concatenate([weight_rows, kernel_padded.reshape(-1, row_width)], axis=0), "ctx"
    )
    shard_rows = weight_rows.shape[0]
    qkv_width = grad_wq.shape[1] + grad_wkv.shape[1]
    grad_qkv = summed[:shard_rows, :qkv_width]
    grad_out = summed[:shard_rows, qkv_width:]
    grad_kernel = summed[shard_rows:].reshape(-1, model_width)[:tap_count]
    return (
        block_out,
        grad_embedded.reshape(recordings, frames_dev, model_width),
        grad_qkv,
        grad_out,
        grad_kernel,
    )


def solution(mesh):
    in_specs = (
        P("dp", "ctx", None),
        P(None, "dp", "ctx"),
        P("dp", None),
        P("dp", None),
        P(),
        P(),
        P(),
        P(),
        P(),
        P("dp", "ctx", None),
    )
    out_specs = (P("dp", "ctx", None), P("dp", "ctx", None), P("dp", None), P("dp", None), P())
    return jax.shard_map(
        on_device, mesh=mesh, in_specs=in_specs, out_specs=out_specs, check_vma=False
    )
```

```python
import jax
import jax.numpy as jnp
from jax import lax
from jax.sharding import PartitionSpec as P

HEADS = 16


EPSILON = 1e-06
NEGATIVE = -1e30


def from_behind(value, axis, steps):
    count = lax.axis_size(axis)
    first, last = (max(0, -steps), min(count, count - steps))
    return lax.ppermute(value, axis, [(source, source + steps) for source in range(first, last)])


def with_halo(block, sides, width):
    for axis, dim in sides:
        count = lax.axis_size(axis)
        forward = [(i, i + 1) for i in range(count - 1)]
        backward = [(target, source) for source, target in forward]
        low = lax.ppermute(
            lax.slice_in_dim(block, block.shape[dim] - width, None, axis=dim), axis, forward
        )
        high = lax.ppermute(lax.slice_in_dim(block, 0, width, axis=dim), axis, backward)
        block = jnp.concatenate([low, block, high], axis=dim)
    return block


def inverse_rms(features):
    return lax.rsqrt(jnp.mean(features * features, axis=-1, keepdims=True) + EPSILON)


def norm_back(features, inverse, gains, upstream):
    inner = jnp.mean(features * gains * upstream, axis=-1, keepdims=True)
    return inverse * gains * upstream - features * inverse * inverse * inverse * inner


def silu_slope(conv_sum):
    sigmoid = jax.nn.sigmoid(conv_sum)
    return sigmoid * (1.0 + conv_sum * (1.0 - sigmoid))


def block_scores(queries, key_block, listed_block, score_scale):
    return jnp.where(
        listed_block,
        jnp.einsum("rqhd,rkhd->rhqk", queries, key_block, preferred_element_type=jnp.float32)
        * score_scale,
        NEGATIVE,
    )


def probabilities(queries, key_part, listed, score_scale):
    pieces = [
        block_scores(queries, key_part[:, position], listed[position], score_scale)
        for position in range(key_part.shape[1])
    ]
    scores = jnp.concatenate(pieces, axis=3)
    highest = jnp.max(scores, axis=3, keepdims=True)
    weights = jnp.exp(scores - highest)
    return weights / jnp.sum(weights, axis=3, keepdims=True)


def on_device(
    ids, tables, w_qkv, w_out, attn_gain, conv_gain, conv_kernel, back_list, ahead_list, cotangent
):
    recordings = ids.shape[0]
    frames_dev = ids.shape[1]
    head_count = HEADS
    tap_count = conv_kernel.shape[0]
    rim_width = (tap_count - 1) // 2
    ids_whole = lax.all_gather(ids, "ctx", axis=1, tiled=True)
    table_whole = lax.all_gather(tables, "dp", axis=1, tiled=True)
    vocab = table_whole.shape[1]
    entries = lax.broadcasted_iota(jnp.int32, (vocab, 1), 0)
    transposed = jnp.zeros((table_whole.shape[2], ids_whole.shape[1]), jnp.float32)
    for codebook in range(table_whole.shape[0]):
        picks = (entries == ids_whole[0, :, codebook][None, :]).astype(jnp.bfloat16)
        transposed = transposed + lax.dot_general(
            table_whole[codebook], picks, (((0,), (0,)), ((), ())),
            preferred_element_type=jnp.float32,
        )
    ctx_count = lax.axis_size("ctx")
    transposed = transposed.astype(jnp.bfloat16).reshape(transposed.shape[0], ctx_count, frames_dev)
    gathered = lax.all_to_all(transposed, "ctx", split_axis=1, concat_axis=0, tiled=True)
    embedded = gathered.reshape(-1, frames_dev).T[None]
    weight_qkv, weight_out = (
        lax.all_gather(w_qkv, "dp", axis=0, tiled=True),
        lax.all_gather(w_out, "dp", axis=0, tiled=True),
    )
    model_width = weight_out.shape[0]
    head_size = model_width // head_count
    score_scale = head_size ** (-0.5)
    features = embedded.astype(jnp.float32).reshape(-1, model_width)
    attn_inverse = inverse_rms(features)
    normed = (features * attn_inverse * attn_gain).astype(jnp.bfloat16)
    projected = jnp.dot(normed, weight_qkv, preferred_element_type=jnp.float32).astype(jnp.bfloat16)
    projected = projected.reshape(recordings, frames_dev, 3 * model_width)
    own_pairs = projected[:, :, model_width:]
    ctx_index = lax.axis_index("ctx")
    back_row = lax.dynamic_index_in_dim(back_list, ctx_index, 0, keepdims=False)
    ahead_row = lax.dynamic_index_in_dim(ahead_list, ctx_index, 0, keepdims=False)
    offsets = [-(step + 1) for step in range(back_list.shape[1])] + [1]
    listed_items = [jnp.array(True)]
    pair_blocks = [own_pairs]
    for offset in offsets:
        list_row = back_row if offset < 0 else ahead_row
        listed_items.append(jnp.any(list_row == ctx_index + offset))
        pair_blocks.append(from_behind(own_pairs, "ctx", -offset))
    listed = jnp.stack(listed_items)
    seen_count = len(pair_blocks)
    stacked = jnp.stack(pair_blocks, axis=1)
    key_all = stacked[..., :model_width].reshape(
        recordings, seen_count, frames_dev, head_count, head_size
    )
    value_all = stacked[..., model_width:].reshape(
        recordings, seen_count, frames_dev, head_count, head_size
    )
    query_all = projected[:, :, :model_width].reshape(recordings, frames_dev, head_count, head_size)

    key_flat = key_all.reshape(recordings, -1, head_count, head_size)
    value_flat = value_all.reshape(recordings, -1, head_count, head_size)
    visible = jnp.repeat(listed, frames_dev)
    scores = jnp.where(
        visible,
        jnp.einsum("rqhd,rkhd->rhqk", query_all, key_flat, preferred_element_type=jnp.float32)
        * score_scale,
        NEGATIVE,
    )
    highest = jnp.max(scores, axis=3, keepdims=True)
    weights = jnp.exp(scores - highest)
    probs = weights / jnp.sum(weights, axis=3, keepdims=True)
    probs_low = probs.astype(jnp.bfloat16)
    mixed = jnp.einsum(
        "rhqk,rkhd->rqhd", probs_low, value_flat, preferred_element_type=jnp.float32
    ).astype(jnp.bfloat16)
    mixed = mixed.reshape(recordings * frames_dev, model_width)
    normed_all, mixed = lax.optimization_barrier(
        (lax.all_gather(normed, "dp", axis=0, tiled=True), mixed)
    )
    projection = jnp.dot(mixed, weight_out, preferred_element_type=jnp.float32)
    middle = (features + projection).astype(jnp.bfloat16)
    middle_wide = middle.astype(jnp.float32)
    conv_inverse = inverse_rms(middle_wide)
    conv_input = (
        (middle_wide * conv_inverse * conv_gain)
        .astype(jnp.bfloat16)
        .reshape(recordings, frames_dev, model_width)
    )
    padded = with_halo(conv_input, (("ctx", 1),), rim_width).astype(jnp.float32)

    conv_sum = jnp.zeros((recordings, frames_dev, model_width), jnp.float32)
    for tap_index in range(tap_count):
        conv_sum = conv_sum + conv_kernel[tap_index] * padded[:, tap_index : tap_index + frames_dev]
    middle_frames = middle_wide.reshape(recordings, frames_dev, model_width)
    block_out = (middle_frames + jax.nn.silu(conv_sum)).astype(jnp.bfloat16)
    upstream = cotangent.astype(jnp.float32)
    grad_conv_low = (upstream * silu_slope(conv_sum)).astype(jnp.bfloat16)
    grad_conv = lax.optimization_barrier(grad_conv_low).astype(jnp.float32)
    grad_padded = with_halo(grad_conv_low, (("ctx", 1),), rim_width).astype(jnp.float32)

    grad_input = jnp.zeros((recordings, frames_dev, model_width), jnp.float32)
    kernel_list = []
    for tap_index in range(tap_count):
        window = padded[:, tap_index : tap_index + frames_dev]
        kernel_list.append(jnp.sum(grad_conv * window, axis=(0, 1)))
        start_row = 2 * rim_width - tap_index
        grad_input = grad_input + conv_kernel[tap_index] * grad_padded[
            :, start_row : start_row + frames_dev
        ]
    kernel_rows = jnp.stack(kernel_list)
    kernel_dp = jnp.sum(lax.all_gather(kernel_rows, "dp"), axis=0)
    grad_middle = (
        upstream.reshape(-1, model_width)
        + norm_back(middle_wide, conv_inverse, conv_gain, grad_input.reshape(-1, model_width))
    ).astype(jnp.bfloat16)
    mixed_all, grad_middle = lax.optimization_barrier(
        (lax.all_gather(mixed, "dp", axis=0, tiled=True), grad_middle)
    )
    contract_rows = (((0,), (0,)), ((), ()))
    contract_columns = (((1,), (1,)), ((), ()))
    grad_mixed = lax.dot_general(
        grad_middle, weight_out, contract_columns, preferred_element_type=jnp.float32
    ).astype(jnp.bfloat16)
    dp_index = lax.axis_index("dp")
    shard_width = model_width // lax.axis_size("dp")
    mixed_columns = lax.dynamic_slice_in_dim(mixed_all, dp_index * shard_width, shard_width, 1)
    middle_rows = lax.all_gather(grad_middle, "dp", axis=0, tiled=True)
    grad_heads = grad_mixed.reshape(recordings, frames_dev, head_count, head_size)

    grad_probs = jnp.einsum(
        "rqhd,rkhd->rhqk", grad_heads, value_flat, preferred_element_type=jnp.float32
    )
    row_sum = jnp.sum(probs * grad_probs, axis=3, keepdims=True)
    grad_scores = (probs * (grad_probs - row_sum) * score_scale).astype(jnp.bfloat16)
    grad_query = jnp.einsum(
        "rhqk,rkhd->rqhd", grad_scores, key_flat, preferred_element_type=jnp.float32
    )
    grad_key_own = jnp.einsum(
        "rhqk,rqhd->rkhd", grad_scores[..., :frames_dev], query_all,
        preferred_element_type=jnp.float32,
    )
    grad_value_own = jnp.einsum(
        "rhqk,rqhd->rkhd", probs_low[..., :frames_dev], grad_heads,
        preferred_element_type=jnp.float32,
    )
    grad_key_far = jnp.einsum(
        "rhqk,rqhd->rkhd", grad_scores[..., frames_dev:], query_all,
        preferred_element_type=jnp.float32,
    ).astype(jnp.bfloat16)
    grad_value_far = jnp.einsum(
        "rhqk,rqhd->rkhd", probs_low[..., frames_dev:], grad_heads,
        preferred_element_type=jnp.float32,
    ).astype(jnp.bfloat16)
    kernel_dp, middle_rows, grad_query = lax.optimization_barrier(
        (kernel_dp, middle_rows, grad_query)
    )
    grad_wout = lax.dot_general(
        mixed_columns, middle_rows, contract_rows, preferred_element_type=jnp.float32
    )
    grad_query = grad_query.reshape(recordings * frames_dev, model_width)
    grad_key_far = grad_key_far.reshape(recordings, seen_count - 1, frames_dev, model_width)
    grad_value_far = grad_value_far.reshape(recordings, seen_count - 1, frames_dev, model_width)
    pair_total = jnp.concatenate(
        [
            grad_key_own.reshape(recordings, frames_dev, model_width),
            grad_value_own.reshape(recordings, frames_dev, model_width),
        ],
        axis=2,
    )
    for position, offset in enumerate(offsets):
        outgoing = jnp.concatenate(
            [grad_key_far[:, position], grad_value_far[:, position]], axis=2
        )
        arrived = from_behind(outgoing, "ctx", offset)
        pair_total = pair_total + arrived.astype(jnp.float32)
    grad_projected = jnp.concatenate(
        [
            grad_query.astype(jnp.bfloat16),
            pair_total.reshape(recordings * frames_dev, 2 * model_width).astype(jnp.bfloat16),
        ],
        axis=1,
    )
    normed_columns = lax.dynamic_slice_in_dim(normed_all, dp_index * shard_width, shard_width, 1)
    query_rows = lax.all_gather(grad_projected[:, :model_width], "dp", axis=0, tiled=True)
    grad_wq = lax.dot_general(
        normed_columns, query_rows, contract_rows, preferred_element_type=jnp.float32
    )
    pair_part = grad_projected[:, model_width:]
    pair_rows = lax.all_gather(pair_part, "dp", axis=0, tiled=True)
    grad_wkv = lax.dot_general(
        normed_columns, pair_rows, contract_rows, preferred_element_type=jnp.float32
    )
    grad_normed = lax.dot_general(
        grad_projected, weight_qkv, contract_columns, preferred_element_type=jnp.float32
    )
    grad_embedded = (
        grad_middle.astype(jnp.float32) + norm_back(features, attn_inverse, attn_gain, grad_normed)
    ).astype(jnp.bfloat16)
    weight_rows = jnp.concatenate([grad_wq, grad_wkv, grad_wout], axis=1)
    row_width = weight_rows.shape[1]
    kernel_padded = jnp.pad(
        kernel_dp, ((0, (-tap_count * model_width) % row_width // model_width), (0, 0))
    )
    summed = lax.psum(
        jnp.concatenate([weight_rows, kernel_padded.reshape(-1, row_width)], axis=0), "ctx"
    )
    shard_rows = weight_rows.shape[0]
    qkv_width = grad_wq.shape[1] + grad_wkv.shape[1]
    grad_qkv = summed[:shard_rows, :qkv_width]
    grad_out = summed[:shard_rows, qkv_width:]
    grad_kernel = summed[shard_rows:].reshape(-1, model_width)[:tap_count]
    return (
        block_out,
        grad_embedded.reshape(recordings, frames_dev, model_width),
        grad_qkv,
        grad_out,
        grad_kernel,
    )


def solution(mesh):
    in_specs = (
        P("dp", "ctx", None),
        P(None, "dp", "ctx"),
        P("dp", None),
        P("dp", None),
        P(),
        P(),
        P(),
        P(),
        P(),
        P("dp", "ctx", None),
    )
    out_specs = (P("dp", "ctx", None), P("dp", "ctx", None), P("dp", None), P("dp", None), P())
    return jax.shard_map(
        on_device, mesh=mesh, in_specs=in_specs, out_specs=out_specs, check_vma=False
    )
```

```python
import jax
import jax.numpy as jnp
from jax import lax
from jax.sharding import PartitionSpec as P

HEADS = 16


EPSILON = 1e-06
NEGATIVE = -1e30


def from_behind(value, axis, steps):
    count = lax.axis_size(axis)
    first, last = (max(0, -steps), min(count, count - steps))
    return lax.ppermute(value, axis, [(source, source + steps) for source in range(first, last)])


def with_halo(block, sides, width):
    for axis, dim in sides:
        count = lax.axis_size(axis)
        forward = [(i, i + 1) for i in range(count - 1)]
        backward = [(target, source) for source, target in forward]
        low = lax.ppermute(
            lax.slice_in_dim(block, block.shape[dim] - width, None, axis=dim), axis, forward
        )
        high = lax.ppermute(lax.slice_in_dim(block, 0, width, axis=dim), axis, backward)
        block = jnp.concatenate([low, block, high], axis=dim)
    return block


def inverse_rms(features):
    return lax.rsqrt(jnp.mean(features * features, axis=-1, keepdims=True) + EPSILON)


def norm_back(features, inverse, gains, upstream):
    inner = jnp.mean(features * gains * upstream, axis=-1, keepdims=True)
    return inverse * gains * upstream - features * inverse * inverse * inverse * inner


def silu_slope(conv_sum):
    sigmoid = jax.nn.sigmoid(conv_sum)
    return sigmoid * (1.0 + conv_sum * (1.0 - sigmoid))


def block_scores(queries, key_block, listed_block, score_scale):
    return jnp.where(
        listed_block,
        jnp.einsum("rqhd,rkhd->rhqk", queries, key_block, preferred_element_type=jnp.float32)
        * score_scale,
        NEGATIVE,
    )


def probabilities(queries, key_part, listed, score_scale):
    pieces = [
        block_scores(queries, key_part[:, position], listed[position], score_scale)
        for position in range(key_part.shape[1])
    ]
    scores = jnp.concatenate(pieces, axis=3)
    highest = jnp.max(scores, axis=3, keepdims=True)
    weights = jnp.exp(scores - highest)
    return weights / jnp.sum(weights, axis=3, keepdims=True)


def on_device(
    ids, tables, w_qkv, w_out, attn_gain, conv_gain, conv_kernel, back_list, ahead_list, cotangent
):
    recordings = ids.shape[0]
    frames_dev = ids.shape[1]
    head_count = HEADS
    tap_count = conv_kernel.shape[0]
    rim_width = (tap_count - 1) // 2
    ids_whole = lax.all_gather(ids, "ctx", axis=1, tiled=True)
    table_whole = lax.all_gather(tables, "dp", axis=1, tiled=True)
    vocab = table_whole.shape[1]
    entries = lax.broadcasted_iota(jnp.int32, (vocab, 1), 0)
    transposed = jnp.zeros((table_whole.shape[2], ids_whole.shape[1]), jnp.float32)
    for codebook in range(table_whole.shape[0]):
        picks = (entries == ids_whole[0, :, codebook][None, :]).astype(jnp.bfloat16)
        transposed = transposed + lax.dot_general(
            table_whole[codebook], picks, (((0,), (0,)), ((), ())),
            preferred_element_type=jnp.float32,
        )
    ctx_count = lax.axis_size("ctx")
    transposed = transposed.astype(jnp.bfloat16).reshape(transposed.shape[0], ctx_count, frames_dev)
    gathered = lax.all_to_all(transposed, "ctx", split_axis=1, concat_axis=0, tiled=True)
    embedded = gathered.reshape(-1, frames_dev).T[None]
    weight_qkv, weight_out = (
        lax.all_gather(w_qkv, "dp", axis=0, tiled=True),
        lax.all_gather(w_out, "dp", axis=0, tiled=True),
    )
    model_width = weight_out.shape[0]
    head_size = model_width // head_count
    score_scale = head_size ** (-0.5)
    features = embedded.astype(jnp.float32).reshape(-1, model_width)
    attn_inverse = inverse_rms(features)
    normed = (features * attn_inverse * attn_gain).astype(jnp.bfloat16)
    projected = jnp.dot(normed, weight_qkv, preferred_element_type=jnp.float32).astype(jnp.bfloat16)
    projected = projected.reshape(recordings, frames_dev, 3 * model_width)
    own_pairs = projected[:, :, model_width:]
    ctx_index = lax.axis_index("ctx")
    back_row = lax.dynamic_index_in_dim(back_list, ctx_index, 0, keepdims=False)
    ahead_row = lax.dynamic_index_in_dim(ahead_list, ctx_index, 0, keepdims=False)
    offsets = [-(step + 1) for step in range(back_list.shape[1])] + [1]
    listed_items = [jnp.array(True)]
    pair_blocks = [own_pairs]
    for offset in offsets:
        list_row = back_row if offset < 0 else ahead_row
        listed_items.append(jnp.any(list_row == ctx_index + offset))
        pair_blocks.append(from_behind(own_pairs, "ctx", -offset))
    listed = jnp.stack(listed_items)
    seen_count = len(pair_blocks)
    stacked = jnp.stack(pair_blocks, axis=1)
    key_all = stacked[..., :model_width].reshape(
        recordings, seen_count, frames_dev, head_count, head_size
    )
    value_all = stacked[..., model_width:].reshape(
        recordings, seen_count, frames_dev, head_count, head_size
    )
    query_all = projected[:, :, :model_width].reshape(recordings, frames_dev, head_count, head_size)

    key_flat = key_all.reshape(recordings, -1, head_count, head_size)
    value_flat = value_all.reshape(recordings, -1, head_count, head_size)
    visible = jnp.repeat(listed, frames_dev)
    scores = jnp.where(
        visible,
        jnp.einsum("rqhd,rkhd->rhqk", query_all, key_flat, preferred_element_type=jnp.float32)
        * score_scale,
        NEGATIVE,
    )
    highest = jnp.max(scores, axis=3, keepdims=True)
    weights = jnp.exp(scores - highest)
    probs = weights / jnp.sum(weights, axis=3, keepdims=True)
    probs_low = probs.astype(jnp.bfloat16)
    mixed = jnp.einsum(
        "rhqk,rkhd->rqhd", probs_low, value_flat, preferred_element_type=jnp.float32
    ).astype(jnp.bfloat16)
    mixed = mixed.reshape(recordings * frames_dev, model_width)
    normed_all, mixed = lax.optimization_barrier(
        (lax.all_gather(normed, "dp", axis=0, tiled=True), mixed)
    )
    projection = jnp.dot(mixed, weight_out, preferred_element_type=jnp.float32)
    middle = (features + projection).astype(jnp.bfloat16)
    middle_wide = middle.astype(jnp.float32)
    conv_inverse = inverse_rms(middle_wide)
    conv_input = (
        (middle_wide * conv_inverse * conv_gain)
        .astype(jnp.bfloat16)
        .reshape(recordings, frames_dev, model_width)
    )
    padded = with_halo(conv_input, (("ctx", 1),), rim_width).astype(jnp.float32)

    conv_sum = jnp.zeros((recordings, frames_dev, model_width), jnp.float32)
    for tap_index in range(tap_count):
        conv_sum = conv_sum + conv_kernel[tap_index] * padded[:, tap_index : tap_index + frames_dev]
    middle_frames = middle_wide.reshape(recordings, frames_dev, model_width)
    block_out = (middle_frames + jax.nn.silu(conv_sum)).astype(jnp.bfloat16)
    upstream = cotangent.astype(jnp.float32)
    grad_conv_low = (upstream * silu_slope(conv_sum)).astype(jnp.bfloat16)
    grad_conv = lax.optimization_barrier(grad_conv_low).astype(jnp.float32)
    grad_padded = with_halo(grad_conv_low, (("ctx", 1),), rim_width).astype(jnp.float32)

    grad_input = jnp.zeros((recordings, frames_dev, model_width), jnp.float32)
    kernel_list = []
    for tap_index in range(tap_count):
        window = padded[:, tap_index : tap_index + frames_dev]
        kernel_list.append(jnp.sum(grad_conv * window, axis=(0, 1)))
        start_row = 2 * rim_width - tap_index
        grad_input = grad_input + conv_kernel[tap_index] * grad_padded[
            :, start_row : start_row + frames_dev
        ]
    kernel_rows = jnp.stack(kernel_list)
    kernel_dp = jnp.sum(lax.all_gather(kernel_rows, "dp"), axis=0)
    grad_middle = (
        upstream.reshape(-1, model_width)
        + norm_back(middle_wide, conv_inverse, conv_gain, grad_input.reshape(-1, model_width))
    ).astype(jnp.bfloat16)
    mixed_all, grad_middle = lax.optimization_barrier(
        (lax.all_gather(mixed, "dp", axis=0, tiled=True), grad_middle)
    )
    contract_rows = (((0,), (0,)), ((), ()))
    contract_columns = (((1,), (1,)), ((), ()))
    grad_mixed = lax.dot_general(
        grad_middle, weight_out, contract_columns, preferred_element_type=jnp.float32
    ).astype(jnp.bfloat16)
    dp_index = lax.axis_index("dp")
    shard_width = model_width // lax.axis_size("dp")
    mixed_columns = lax.dynamic_slice_in_dim(mixed_all, dp_index * shard_width, shard_width, 1)
    middle_rows = lax.all_gather(grad_middle, "dp", axis=0, tiled=True)
    grad_heads = grad_mixed.reshape(recordings, frames_dev, head_count, head_size)

    grad_probs = jnp.einsum(
        "rqhd,rkhd->rhqk", grad_heads, value_flat, preferred_element_type=jnp.float32
    )
    row_sum = jnp.sum(probs * grad_probs, axis=3, keepdims=True)
    grad_scores = (probs * (grad_probs - row_sum) * score_scale).astype(jnp.bfloat16)
    grad_query = jnp.einsum(
        "rhqk,rkhd->rqhd", grad_scores, key_flat, preferred_element_type=jnp.float32
    )
    grad_key_own = jnp.einsum(
        "rhqk,rqhd->rkhd", grad_scores[..., :frames_dev], query_all,
        preferred_element_type=jnp.float32,
    )
    grad_value_own = jnp.einsum(
        "rhqk,rqhd->rkhd", probs_low[..., :frames_dev], grad_heads,
        preferred_element_type=jnp.float32,
    )
    grad_key_far = jnp.einsum(
        "rhqk,rqhd->rkhd", grad_scores[..., frames_dev:], query_all,
        preferred_element_type=jnp.float32,
    ).astype(jnp.bfloat16)
    grad_value_far = jnp.einsum(
        "rhqk,rqhd->rkhd", probs_low[..., frames_dev:], grad_heads,
        preferred_element_type=jnp.float32,
    ).astype(jnp.bfloat16)
    kernel_dp, middle_rows, grad_query = lax.optimization_barrier(
        (kernel_dp, middle_rows, grad_query)
    )
    grad_wout = lax.dot_general(
        mixed_columns, middle_rows, contract_rows, preferred_element_type=jnp.float32
    )
    grad_query = grad_query.reshape(recordings * frames_dev, model_width)
    grad_key_far = grad_key_far.reshape(recordings, seen_count - 1, frames_dev, model_width)
    grad_value_far = grad_value_far.reshape(recordings, seen_count - 1, frames_dev, model_width)
    pair_total = jnp.concatenate(
        [
            grad_key_own.reshape(recordings, frames_dev, model_width),
            grad_value_own.reshape(recordings, frames_dev, model_width),
        ],
        axis=2,
    )
    for position, offset in enumerate(offsets):
        outgoing = jnp.concatenate(
            [grad_key_far[:, position], grad_value_far[:, position]], axis=2
        )
        arrived = from_behind(outgoing, "ctx", offset)
        pair_total = pair_total + arrived.astype(jnp.float32)
    grad_projected = jnp.concatenate(
        [
            grad_query.astype(jnp.bfloat16),
            pair_total.reshape(recordings * frames_dev, 2 * model_width).astype(jnp.bfloat16),
        ],
        axis=1,
    )
    normed_columns = lax.dynamic_slice_in_dim(normed_all, dp_index * shard_width, shard_width, 1)
    query_rows = lax.all_gather(grad_projected[:, :model_width], "dp", axis=0, tiled=True)
    grad_wq = lax.dot_general(
        normed_columns, query_rows, contract_rows, preferred_element_type=jnp.float32
    )
    pair_part = grad_projected[:, model_width:]
    pair_rows = lax.all_gather(pair_part, "dp", axis=0, tiled=True)
    grad_wkv = lax.dot_general(
        normed_columns, pair_rows, contract_rows, preferred_element_type=jnp.float32
    )
    grad_normed = lax.dot_general(
        grad_projected, weight_qkv, contract_columns, preferred_element_type=jnp.float32
    )
    grad_embedded = (
        grad_middle.astype(jnp.float32) + norm_back(features, attn_inverse, attn_gain, grad_normed)
    ).astype(jnp.bfloat16)
    weight_rows = jnp.concatenate([grad_wq, grad_wkv, grad_wout], axis=1)
    row_width = weight_rows.shape[1]
    kernel_padded = jnp.pad(
        kernel_dp, ((0, (-tap_count * model_width) % row_width // model_width), (0, 0))
    )
    packed = jnp.concatenate([weight_rows, kernel_padded.reshape(-1, row_width)], axis=0)
    summed = lax.all_gather(
        lax.psum_scatter(packed, "ctx", scatter_dimension=1, tiled=True), "ctx", axis=1, tiled=True
    )
    shard_rows = weight_rows.shape[0]
    qkv_width = grad_wq.shape[1] + grad_wkv.shape[1]
    grad_qkv = summed[:shard_rows, :qkv_width]
    grad_out = summed[:shard_rows, qkv_width:]
    grad_kernel = summed[shard_rows:].reshape(-1, model_width)[:tap_count]
    return (
        block_out,
        grad_embedded.reshape(recordings, frames_dev, model_width),
        grad_qkv,
        grad_out,
        grad_kernel,
    )


def solution(mesh):
    in_specs = (
        P("dp", "ctx", None),
        P(None, "dp", "ctx"),
        P("dp", None),
        P("dp", None),
        P(),
        P(),
        P(),
        P(),
        P(),
        P("dp", "ctx", None),
    )
    out_specs = (P("dp", "ctx", None), P("dp", "ctx", None), P("dp", None), P("dp", None), P())
    return jax.shard_map(
        on_device, mesh=mesh, in_specs=in_specs, out_specs=out_specs, check_vma=False
    )
```

```python
import jax
import jax.numpy as jnp
from jax import lax
from jax.sharding import PartitionSpec as P

HEADS = 16


EPSILON = 1e-06
NEGATIVE = -1e30


def from_behind(value, axis, steps):
    count = lax.axis_size(axis)
    first, last = (max(0, -steps), min(count, count - steps))
    return lax.ppermute(value, axis, [(source, source + steps) for source in range(first, last)])


def with_halo(block, sides, width):
    for axis, dim in sides:
        count = lax.axis_size(axis)
        forward = [(i, i + 1) for i in range(count - 1)]
        backward = [(target, source) for source, target in forward]
        low = lax.ppermute(
            lax.slice_in_dim(block, block.shape[dim] - width, None, axis=dim), axis, forward
        )
        high = lax.ppermute(lax.slice_in_dim(block, 0, width, axis=dim), axis, backward)
        block = jnp.concatenate([low, block, high], axis=dim)
    return block


def inverse_rms(features):
    return lax.rsqrt(jnp.mean(features * features, axis=-1, keepdims=True) + EPSILON)


def norm_back(features, inverse, gains, upstream):
    inner = jnp.mean(features * gains * upstream, axis=-1, keepdims=True)
    return inverse * gains * upstream - features * inverse * inverse * inverse * inner


def silu_slope(conv_sum):
    sigmoid = jax.nn.sigmoid(conv_sum)
    return sigmoid * (1.0 + conv_sum * (1.0 - sigmoid))


def block_scores(queries, key_block, listed_block, score_scale):
    return jnp.where(
        listed_block,
        jnp.einsum("rqhd,rkhd->rhqk", queries, key_block, preferred_element_type=jnp.float32)
        * score_scale,
        NEGATIVE,
    )


def probabilities(queries, key_part, listed, score_scale):
    pieces = [
        block_scores(queries, key_part[:, position], listed[position], score_scale)
        for position in range(key_part.shape[1])
    ]
    scores = jnp.concatenate(pieces, axis=3)
    highest = jnp.max(scores, axis=3, keepdims=True)
    weights = jnp.exp(scores - highest)
    return weights / jnp.sum(weights, axis=3, keepdims=True)


def on_device(
    ids, tables, w_qkv, w_out, attn_gain, conv_gain, conv_kernel, back_list, ahead_list, cotangent
):
    recordings = ids.shape[0]
    frames_dev = ids.shape[1]
    head_count = HEADS
    tap_count = conv_kernel.shape[0]
    rim_width = (tap_count - 1) // 2
    ids_whole = lax.all_gather(ids, "ctx", axis=1, tiled=True)
    table_whole = lax.all_gather(tables, "dp", axis=1, tiled=True)
    vocab = table_whole.shape[1]
    entries = lax.broadcasted_iota(jnp.int32, (vocab, 1), 0)
    transposed = jnp.zeros((table_whole.shape[2], ids_whole.shape[1]), jnp.float32)
    for codebook in range(table_whole.shape[0]):
        picks = (entries == ids_whole[0, :, codebook][None, :]).astype(jnp.bfloat16)
        transposed = transposed + lax.dot_general(
            table_whole[codebook], picks, (((0,), (0,)), ((), ())),
            preferred_element_type=jnp.float32,
        )
    ctx_count = lax.axis_size("ctx")
    transposed = transposed.astype(jnp.bfloat16).reshape(transposed.shape[0], ctx_count, frames_dev)
    gathered = lax.all_to_all(transposed, "ctx", split_axis=1, concat_axis=0, tiled=True)
    embedded = gathered.reshape(-1, frames_dev).T[None]
    weight_qkv, weight_out = (
        lax.all_gather(w_qkv, "dp", axis=0, tiled=True),
        lax.all_gather(w_out, "dp", axis=0, tiled=True),
    )
    model_width = weight_out.shape[0]
    head_size = model_width // head_count
    score_scale = head_size ** (-0.5)
    features = embedded.astype(jnp.float32).reshape(-1, model_width)
    attn_inverse = inverse_rms(features)
    normed = (features * attn_inverse * attn_gain).astype(jnp.bfloat16)
    projected = jnp.dot(normed, weight_qkv, preferred_element_type=jnp.float32).astype(jnp.bfloat16)
    projected = projected.reshape(recordings, frames_dev, 3 * model_width)
    own_pairs = projected[:, :, model_width:]
    ctx_index = lax.axis_index("ctx")
    back_row = lax.dynamic_index_in_dim(back_list, ctx_index, 0, keepdims=False)
    ahead_row = lax.dynamic_index_in_dim(ahead_list, ctx_index, 0, keepdims=False)
    offsets = [-(step + 1) for step in range(back_list.shape[1])] + [1]
    listed_items = [jnp.array(True)]
    pair_blocks = [own_pairs]
    for offset in offsets:
        list_row = back_row if offset < 0 else ahead_row
        listed_items.append(jnp.any(list_row == ctx_index + offset))
        pair_blocks.append(from_behind(own_pairs, "ctx", -offset))
    listed = jnp.stack(listed_items)
    seen_count = len(pair_blocks)
    stacked = jnp.stack(pair_blocks, axis=1)
    key_all = stacked[..., :model_width].reshape(
        recordings, seen_count, frames_dev, head_count, head_size
    )
    value_all = stacked[..., model_width:].reshape(
        recordings, seen_count, frames_dev, head_count, head_size
    )
    query_all = projected[:, :, :model_width].reshape(recordings, frames_dev, head_count, head_size)

    key_flat = key_all.reshape(recordings, -1, head_count, head_size)
    value_flat = value_all.reshape(recordings, -1, head_count, head_size)
    visible = jnp.repeat(listed, frames_dev)
    scores = jnp.where(
        visible,
        jnp.einsum("rqhd,rkhd->rhqk", query_all, key_flat, preferred_element_type=jnp.float32)
        * score_scale,
        NEGATIVE,
    )
    highest = jnp.max(scores, axis=3, keepdims=True)
    weights = jnp.exp(scores - highest)
    probs = weights / jnp.sum(weights, axis=3, keepdims=True)
    probs_low = probs.astype(jnp.bfloat16)
    mixed = jnp.einsum(
        "rhqk,rkhd->rqhd", probs_low, value_flat, preferred_element_type=jnp.float32
    ).astype(jnp.bfloat16)
    mixed = mixed.reshape(recordings * frames_dev, model_width)
    normed_all, mixed = lax.optimization_barrier(
        (lax.all_gather(normed, "dp", axis=0, tiled=True), mixed)
    )
    projection = jnp.dot(mixed, weight_out, preferred_element_type=jnp.float32)
    middle = (features + projection).astype(jnp.bfloat16)
    middle_wide = middle.astype(jnp.float32)
    conv_inverse = inverse_rms(middle_wide)
    conv_input = (
        (middle_wide * conv_inverse * conv_gain)
        .astype(jnp.bfloat16)
        .reshape(recordings, frames_dev, model_width)
    )
    padded = with_halo(conv_input, (("ctx", 1),), rim_width).astype(jnp.float32)

    conv_sum = jnp.zeros((recordings, frames_dev, model_width), jnp.float32)
    for tap_index in range(tap_count):
        conv_sum = conv_sum + conv_kernel[tap_index] * padded[:, tap_index : tap_index + frames_dev]
    middle_frames = middle_wide.reshape(recordings, frames_dev, model_width)
    block_out = (middle_frames + jax.nn.silu(conv_sum)).astype(jnp.bfloat16)
    upstream = cotangent.astype(jnp.float32)
    grad_conv_low = (upstream * silu_slope(conv_sum)).astype(jnp.bfloat16)
    grad_conv = lax.optimization_barrier(grad_conv_low).astype(jnp.float32)
    grad_padded = with_halo(grad_conv_low, (("ctx", 1),), rim_width).astype(jnp.float32)

    grad_input = jnp.zeros((recordings, frames_dev, model_width), jnp.float32)
    kernel_list = []
    for tap_index in range(tap_count):
        window = padded[:, tap_index : tap_index + frames_dev]
        kernel_list.append(jnp.sum(grad_conv * window, axis=(0, 1)))
        start_row = 2 * rim_width - tap_index
        grad_input = grad_input + conv_kernel[tap_index] * grad_padded[
            :, start_row : start_row + frames_dev
        ]
    kernel_rows = jnp.stack(kernel_list)
    kernel_dp = jnp.sum(lax.all_gather(kernel_rows, "dp"), axis=0)
    grad_middle = (
        upstream.reshape(-1, model_width)
        + norm_back(middle_wide, conv_inverse, conv_gain, grad_input.reshape(-1, model_width))
    ).astype(jnp.bfloat16)
    mixed_all, grad_middle = lax.optimization_barrier(
        (lax.all_gather(mixed, "dp", axis=0, tiled=True), grad_middle)
    )
    contract_rows = (((0,), (0,)), ((), ()))
    contract_columns = (((1,), (1,)), ((), ()))
    grad_mixed = lax.dot_general(
        grad_middle, weight_out, contract_columns, preferred_element_type=jnp.float32
    ).astype(jnp.bfloat16)
    dp_index = lax.axis_index("dp")
    shard_width = model_width // lax.axis_size("dp")
    mixed_columns = lax.dynamic_slice_in_dim(mixed_all, dp_index * shard_width, shard_width, 1)
    middle_rows = lax.all_gather(grad_middle, "dp", axis=0, tiled=True)
    grad_heads = grad_mixed.reshape(recordings, frames_dev, head_count, head_size)

    grad_probs = jnp.einsum(
        "rqhd,rkhd->rhqk", grad_heads, value_flat, preferred_element_type=jnp.float32
    )
    row_sum = jnp.sum(probs * grad_probs, axis=3, keepdims=True)
    grad_scores = (probs * (grad_probs - row_sum) * score_scale).astype(jnp.bfloat16)
    grad_query = jnp.einsum(
        "rhqk,rkhd->rqhd", grad_scores, key_flat, preferred_element_type=jnp.float32
    )
    transposed_dims = (((1,), (2,)), ((0, 2), (0, 1)))
    key_grads = lax.dot_general(
        query_all, grad_scores, transposed_dims, preferred_element_type=jnp.float32
    ).reshape(recordings, model_width, -1)
    value_grads = lax.dot_general(
        grad_heads, probs_low, transposed_dims, preferred_element_type=jnp.float32
    ).reshape(recordings, model_width, -1)
    kernel_dp, middle_rows, grad_query = lax.optimization_barrier(
        (kernel_dp, middle_rows, grad_query)
    )
    grad_wout = lax.dot_general(
        mixed_columns, middle_rows, contract_rows, preferred_element_type=jnp.float32
    )
    grad_query = grad_query.reshape(recordings * frames_dev, model_width).astype(jnp.bfloat16)
    pair_total = jnp.concatenate(
        [key_grads[:, :, :frames_dev], value_grads[:, :, :frames_dev]], axis=1
    )
    for position, offset in enumerate(offsets):
        window = slice((position + 1) * frames_dev, (position + 2) * frames_dev)
        outgoing = jnp.concatenate(
            [key_grads[:, :, window], value_grads[:, :, window]], axis=1
        ).astype(jnp.bfloat16)
        arrived = from_behind(outgoing, "ctx", offset)
        pair_total = pair_total + arrived.astype(jnp.float32)
    pair_low = pair_total.astype(jnp.bfloat16)
    normed_columns = lax.dynamic_slice_in_dim(normed_all, dp_index * shard_width, shard_width, 1)
    query_rows = lax.all_gather(grad_query, "dp", axis=0, tiled=True)
    grad_wq = lax.dot_general(
        normed_columns, query_rows, contract_rows, preferred_element_type=jnp.float32
    )
    pair_rows = lax.all_gather(pair_low, "dp", axis=0, tiled=True)
    grad_wkv = jnp.einsum(
        "nfc,nkf->ck",
        normed_columns.reshape(pair_rows.shape[0], frames_dev, shard_width),
        pair_rows,
        preferred_element_type=jnp.float32,
    )
    grad_normed = lax.dot_general(
        grad_query, weight_qkv[:, :model_width], contract_columns,
        preferred_element_type=jnp.float32,
    ) + jnp.einsum(
        "rkf,ik->rfi", pair_low, weight_qkv[:, model_width:], preferred_element_type=jnp.float32
    ).reshape(recordings * frames_dev, model_width)
    grad_embedded = (
        grad_middle.astype(jnp.float32) + norm_back(features, attn_inverse, attn_gain, grad_normed)
    ).astype(jnp.bfloat16)
    weight_rows = jnp.concatenate([grad_wq, grad_wkv, grad_wout], axis=1)
    row_width = weight_rows.shape[1]
    kernel_padded = jnp.pad(
        kernel_dp, ((0, (-tap_count * model_width) % row_width // model_width), (0, 0))
    )
    summed = lax.psum(
        jnp.concatenate([weight_rows, kernel_padded.reshape(-1, row_width)], axis=0), "ctx"
    )
    shard_rows = weight_rows.shape[0]
    qkv_width = grad_wq.shape[1] + grad_wkv.shape[1]
    grad_qkv = summed[:shard_rows, :qkv_width]
    grad_out = summed[:shard_rows, qkv_width:]
    grad_kernel = summed[shard_rows:].reshape(-1, model_width)[:tap_count]
    return (
        block_out,
        grad_embedded.reshape(recordings, frames_dev, model_width),
        grad_qkv,
        grad_out,
        grad_kernel,
    )


def solution(mesh):
    in_specs = (
        P("dp", "ctx", None),
        P(None, "dp", "ctx"),
        P("dp", None),
        P("dp", None),
        P(),
        P(),
        P(),
        P(),
        P(),
        P("dp", "ctx", None),
    )
    out_specs = (P("dp", "ctx", None), P("dp", "ctx", None), P("dp", None), P("dp", None), P())
    return jax.shard_map(
        on_device, mesh=mesh, in_specs=in_specs, out_specs=out_specs, check_vma=False
    )
```

```python
import jax
import jax.numpy as jnp
from jax import lax
from jax.sharding import PartitionSpec as P

HEADS = 16


EPSILON = 1e-06
NEGATIVE = -1e30


def from_behind(value, axis, steps):
    count = lax.axis_size(axis)
    first, last = (max(0, -steps), min(count, count - steps))
    return lax.ppermute(value, axis, [(source, source + steps) for source in range(first, last)])


def with_halo(block, sides, width):
    for axis, dim in sides:
        count = lax.axis_size(axis)
        forward = [(i, i + 1) for i in range(count - 1)]
        backward = [(target, source) for source, target in forward]
        low = lax.ppermute(
            lax.slice_in_dim(block, block.shape[dim] - width, None, axis=dim), axis, forward
        )
        high = lax.ppermute(lax.slice_in_dim(block, 0, width, axis=dim), axis, backward)
        block = jnp.concatenate([low, block, high], axis=dim)
    return block


def inverse_rms(features):
    return lax.rsqrt(jnp.mean(features * features, axis=-1, keepdims=True) + EPSILON)


def norm_back(features, inverse, gains, upstream):
    inner = jnp.mean(features * gains * upstream, axis=-1, keepdims=True)
    return inverse * gains * upstream - features * inverse * inverse * inverse * inner


def silu_slope(conv_sum):
    sigmoid = jax.nn.sigmoid(conv_sum)
    return sigmoid * (1.0 + conv_sum * (1.0 - sigmoid))


def block_scores(queries, key_block, listed_block, score_scale):
    return jnp.where(
        listed_block,
        jnp.einsum("rqhd,rkhd->rhqk", queries, key_block, preferred_element_type=jnp.float32)
        * score_scale,
        NEGATIVE,
    )


def probabilities(queries, key_part, listed, score_scale):
    pieces = [
        block_scores(queries, key_part[:, position], listed[position], score_scale)
        for position in range(key_part.shape[1])
    ]
    scores = jnp.concatenate(pieces, axis=3)
    highest = jnp.max(scores, axis=3, keepdims=True)
    weights = jnp.exp(scores - highest)
    return weights / jnp.sum(weights, axis=3, keepdims=True)


def on_device(
    ids, tables, w_qkv, w_out, attn_gain, conv_gain, conv_kernel, back_list, ahead_list, cotangent
):
    recordings = ids.shape[0]
    frames_dev = ids.shape[1]
    head_count = HEADS
    tap_count = conv_kernel.shape[0]
    rim_width = (tap_count - 1) // 2
    ids_whole = lax.all_gather(ids, "ctx", axis=1, tiled=True)
    table_whole = lax.all_gather(tables, "dp", axis=1, tiled=True)
    vocab = table_whole.shape[1]
    entries = lax.broadcasted_iota(jnp.int32, (vocab, 1), 0)
    transposed = jnp.zeros((table_whole.shape[2], ids_whole.shape[1]), jnp.float32)
    for codebook in range(table_whole.shape[0]):
        picks = (entries == ids_whole[0, :, codebook][None, :]).astype(jnp.bfloat16)
        transposed = transposed + lax.dot_general(
            table_whole[codebook], picks, (((0,), (0,)), ((), ())),
            preferred_element_type=jnp.float32,
        )
    ctx_count = lax.axis_size("ctx")
    transposed = transposed.astype(jnp.bfloat16).reshape(transposed.shape[0], ctx_count, frames_dev)
    gathered = lax.all_to_all(transposed, "ctx", split_axis=1, concat_axis=0, tiled=True)
    embedded = gathered.reshape(-1, frames_dev).T[None]
    weight_qkv, weight_out = (
        lax.all_gather(w_qkv, "dp", axis=0, tiled=True),
        lax.all_gather(w_out, "dp", axis=0, tiled=True),
    )
    model_width = weight_out.shape[0]
    head_size = model_width // head_count
    score_scale = head_size ** (-0.5)
    features = embedded.astype(jnp.float32).reshape(-1, model_width)
    attn_inverse = inverse_rms(features)
    normed = (features * attn_inverse * attn_gain).astype(jnp.bfloat16)
    projected = jnp.dot(normed, weight_qkv, preferred_element_type=jnp.float32).astype(jnp.bfloat16)
    projected = projected.reshape(recordings, frames_dev, 3 * model_width)
    own_pairs = projected[:, :, model_width:]
    ctx_index = lax.axis_index("ctx")
    back_row = lax.dynamic_index_in_dim(back_list, ctx_index, 0, keepdims=False)
    ahead_row = lax.dynamic_index_in_dim(ahead_list, ctx_index, 0, keepdims=False)
    offsets = [-(step + 1) for step in range(back_list.shape[1])] + [1]
    listed_items = [jnp.array(True)]
    pair_blocks = [own_pairs]
    for offset in offsets:
        list_row = back_row if offset < 0 else ahead_row
        listed_items.append(jnp.any(list_row == ctx_index + offset))
        pair_blocks.append(from_behind(own_pairs, "ctx", -offset))
    listed = jnp.stack(listed_items)
    seen_count = len(pair_blocks)
    stacked = jnp.stack(pair_blocks, axis=1)
    key_all = stacked[..., :model_width].reshape(
        recordings, seen_count, frames_dev, head_count, head_size
    )
    value_all = stacked[..., model_width:].reshape(
        recordings, seen_count, frames_dev, head_count, head_size
    )
    query_all = projected[:, :, :model_width].reshape(recordings, frames_dev, head_count, head_size)

    key_flat = key_all.reshape(recordings, -1, head_count, head_size)
    value_flat = value_all.reshape(recordings, -1, head_count, head_size)
    visible = jnp.repeat(listed, frames_dev)
    scores = jnp.where(
        visible,
        jnp.einsum("rqhd,rkhd->rhqk", query_all, key_flat, preferred_element_type=jnp.float32)
        * score_scale,
        NEGATIVE,
    )
    highest = jnp.max(scores, axis=3, keepdims=True)
    weights = jnp.exp(scores - highest)
    probs = weights / jnp.sum(weights, axis=3, keepdims=True)
    probs_low = probs.astype(jnp.bfloat16)
    mixed = jnp.einsum(
        "rhqk,rkhd->rqhd", probs_low, value_flat, preferred_element_type=jnp.float32
    ).astype(jnp.bfloat16)
    mixed = mixed.reshape(recordings * frames_dev, model_width)
    normed_all, mixed = lax.optimization_barrier(
        (lax.all_gather(normed, "dp", axis=0, tiled=True), mixed)
    )
    projection = jnp.dot(mixed, weight_out, preferred_element_type=jnp.float32)
    middle = (features + projection).astype(jnp.bfloat16)
    middle_wide = middle.astype(jnp.float32)
    conv_inverse = inverse_rms(middle_wide)
    conv_input = (
        (middle_wide * conv_inverse * conv_gain)
        .astype(jnp.bfloat16)
        .reshape(recordings, frames_dev, model_width)
    )
    padded = with_halo(conv_input, (("ctx", 1),), rim_width).astype(jnp.float32)

    conv_sum = jnp.zeros((recordings, frames_dev, model_width), jnp.float32)
    for tap_index in range(tap_count):
        conv_sum = conv_sum + conv_kernel[tap_index] * padded[:, tap_index : tap_index + frames_dev]
    middle_frames = middle_wide.reshape(recordings, frames_dev, model_width)
    block_out = (middle_frames + jax.nn.silu(conv_sum)).astype(jnp.bfloat16)
    upstream = cotangent.astype(jnp.float32)
    grad_conv_low = (upstream * silu_slope(conv_sum)).astype(jnp.bfloat16)
    grad_conv = lax.optimization_barrier(grad_conv_low).astype(jnp.float32)
    grad_padded = with_halo(grad_conv_low, (("ctx", 1),), rim_width).astype(jnp.float32)

    grad_input = jnp.zeros((recordings, frames_dev, model_width), jnp.float32)
    kernel_list = []
    for tap_index in range(tap_count):
        window = padded[:, tap_index : tap_index + frames_dev]
        kernel_list.append(jnp.sum(grad_conv * window, axis=(0, 1)))
        start_row = 2 * rim_width - tap_index
        grad_input = grad_input + conv_kernel[tap_index] * grad_padded[
            :, start_row : start_row + frames_dev
        ]
    kernel_rows = jnp.stack(kernel_list)
    kernel_dp = jnp.sum(lax.all_gather(kernel_rows, "dp"), axis=0)
    grad_middle = (
        upstream.reshape(-1, model_width)
        + norm_back(middle_wide, conv_inverse, conv_gain, grad_input.reshape(-1, model_width))
    ).astype(jnp.bfloat16)
    mixed_all, grad_middle = lax.optimization_barrier(
        (lax.all_gather(mixed, "dp", axis=0, tiled=True), grad_middle)
    )
    contract_rows = (((0,), (0,)), ((), ()))
    contract_columns = (((1,), (1,)), ((), ()))
    grad_mixed = lax.dot_general(
        grad_middle, weight_out, contract_columns, preferred_element_type=jnp.float32
    ).astype(jnp.bfloat16)
    dp_index = lax.axis_index("dp")
    shard_width = model_width // lax.axis_size("dp")
    mixed_columns = lax.dynamic_slice_in_dim(mixed_all, dp_index * shard_width, shard_width, 1)
    middle_rows = lax.all_gather(grad_middle, "dp", axis=0, tiled=True)
    grad_heads = grad_mixed.reshape(recordings, frames_dev, head_count, head_size)

    grad_probs = jnp.einsum(
        "rqhd,rkhd->rhqk", grad_heads, value_flat, preferred_element_type=jnp.float32
    )
    row_sum = jnp.sum(probs * grad_probs, axis=3, keepdims=True)
    grad_scores = lax.optimization_barrier(
        (probs * (grad_probs - row_sum) * score_scale).astype(jnp.bfloat16)
    )
    transposed_dims = (((1,), (2,)), ((0, 2), (0, 1)))
    key_grads = lax.dot_general(
        query_all, grad_scores, transposed_dims, preferred_element_type=jnp.float32
    ).reshape(recordings, model_width, -1)
    value_grads = lax.dot_general(
        grad_heads, probs_low, transposed_dims, preferred_element_type=jnp.float32
    ).reshape(recordings, model_width, -1)
    outgoing = [
        jnp.concatenate(
            [key_grads[:, :, window], value_grads[:, :, window]], axis=1
        ).astype(jnp.bfloat16)
        for window in [
            slice((position + 1) * frames_dev, (position + 2) * frames_dev)
            for position in range(len(offsets))
        ]
    ]
    outgoing, scores_for_query = lax.optimization_barrier((outgoing, grad_scores))
    arrivals = [from_behind(sent, "ctx", offset) for sent, offset in zip(outgoing, offsets)]
    grad_query = jnp.einsum(
        "rhqk,rkhd->rqhd", scores_for_query, key_flat, preferred_element_type=jnp.float32
    )
    kernel_dp, middle_rows, grad_query = lax.optimization_barrier(
        (kernel_dp, middle_rows, grad_query)
    )
    grad_wout = lax.dot_general(
        mixed_columns, middle_rows, contract_rows, preferred_element_type=jnp.float32
    )
    grad_query = grad_query.reshape(recordings * frames_dev, model_width).astype(jnp.bfloat16)
    pair_total = jnp.concatenate(
        [key_grads[:, :, :frames_dev], value_grads[:, :, :frames_dev]], axis=1
    )
    for arrived in arrivals:
        pair_total = pair_total + arrived.astype(jnp.float32)
    pair_low = pair_total.astype(jnp.bfloat16)
    normed_columns = lax.dynamic_slice_in_dim(normed_all, dp_index * shard_width, shard_width, 1)
    query_rows = lax.all_gather(grad_query, "dp", axis=0, tiled=True)
    grad_wq = lax.dot_general(
        normed_columns, query_rows, contract_rows, preferred_element_type=jnp.float32
    )
    pair_rows = lax.all_gather(pair_low, "dp", axis=0, tiled=True)
    grad_wkv = jnp.einsum(
        "nfc,nkf->ck",
        normed_columns.reshape(pair_rows.shape[0], frames_dev, shard_width),
        pair_rows,
        preferred_element_type=jnp.float32,
    )
    grad_normed = lax.dot_general(
        grad_query, weight_qkv[:, :model_width], contract_columns,
        preferred_element_type=jnp.float32,
    ) + jnp.einsum(
        "rkf,ik->rfi", pair_low, weight_qkv[:, model_width:], preferred_element_type=jnp.float32
    ).reshape(recordings * frames_dev, model_width)
    grad_embedded = (
        grad_middle.astype(jnp.float32) + norm_back(features, attn_inverse, attn_gain, grad_normed)
    ).astype(jnp.bfloat16)
    weight_rows = jnp.concatenate([grad_wq, grad_wkv, grad_wout], axis=1)
    row_width = weight_rows.shape[1]
    kernel_padded = jnp.pad(
        kernel_dp, ((0, (-tap_count * model_width) % row_width // model_width), (0, 0))
    )
    summed = lax.psum(
        jnp.concatenate([weight_rows, kernel_padded.reshape(-1, row_width)], axis=0), "ctx"
    )
    shard_rows = weight_rows.shape[0]
    qkv_width = grad_wq.shape[1] + grad_wkv.shape[1]
    grad_qkv = summed[:shard_rows, :qkv_width]
    grad_out = summed[:shard_rows, qkv_width:]
    grad_kernel = summed[shard_rows:].reshape(-1, model_width)[:tap_count]
    return (
        block_out,
        grad_embedded.reshape(recordings, frames_dev, model_width),
        grad_qkv,
        grad_out,
        grad_kernel,
    )


def solution(mesh):
    in_specs = (
        P("dp", "ctx", None),
        P(None, "dp", "ctx"),
        P("dp", None),
        P("dp", None),
        P(),
        P(),
        P(),
        P(),
        P(),
        P("dp", "ctx", None),
    )
    out_specs = (P("dp", "ctx", None), P("dp", "ctx", None), P("dp", None), P("dp", None), P())
    return jax.shard_map(
        on_device, mesh=mesh, in_specs=in_specs, out_specs=out_specs, check_vma=False
    )
```

```python
import jax
import jax.numpy as jnp
from jax import lax
from jax.sharding import PartitionSpec as P

HEADS = 16


EPSILON = 1e-06
NEGATIVE = -1e30


def from_behind(value, axis, steps):
    count = lax.axis_size(axis)
    first, last = (max(0, -steps), min(count, count - steps))
    return lax.ppermute(value, axis, [(source, source + steps) for source in range(first, last)])


def with_halo(block, sides, width):
    for axis, dim in sides:
        count = lax.axis_size(axis)
        forward = [(i, i + 1) for i in range(count - 1)]
        backward = [(target, source) for source, target in forward]
        low = lax.ppermute(
            lax.slice_in_dim(block, block.shape[dim] - width, None, axis=dim), axis, forward
        )
        high = lax.ppermute(lax.slice_in_dim(block, 0, width, axis=dim), axis, backward)
        block = jnp.concatenate([low, block, high], axis=dim)
    return block


def inverse_rms(features):
    return lax.rsqrt(jnp.mean(features * features, axis=-1, keepdims=True) + EPSILON)


def norm_back(features, inverse, gains, upstream):
    inner = jnp.mean(features * gains * upstream, axis=-1, keepdims=True)
    return inverse * gains * upstream - features * inverse * inverse * inverse * inner


def silu_slope(conv_sum):
    sigmoid = jax.nn.sigmoid(conv_sum)
    return sigmoid * (1.0 + conv_sum * (1.0 - sigmoid))


def block_scores(queries, key_block, listed_block, score_scale):
    return jnp.where(
        listed_block,
        jnp.einsum("rqhd,rkhd->rhqk", queries, key_block, preferred_element_type=jnp.float32)
        * score_scale,
        NEGATIVE,
    )


def probabilities(queries, key_part, listed, score_scale):
    pieces = [
        block_scores(queries, key_part[:, position], listed[position], score_scale)
        for position in range(key_part.shape[1])
    ]
    scores = jnp.concatenate(pieces, axis=3)
    highest = jnp.max(scores, axis=3, keepdims=True)
    weights = jnp.exp(scores - highest)
    return weights / jnp.sum(weights, axis=3, keepdims=True)


def on_device(
    ids, tables, w_qkv, w_out, attn_gain, conv_gain, conv_kernel, back_list, ahead_list, cotangent
):
    recordings = ids.shape[0]
    frames_dev = ids.shape[1]
    head_count = HEADS
    tap_count = conv_kernel.shape[0]
    rim_width = (tap_count - 1) // 2
    ids_whole = lax.all_gather(ids, "ctx", axis=1, tiled=True)
    table_whole = lax.all_gather(tables, "dp", axis=1, tiled=True)
    vocab = table_whole.shape[1]
    entries = lax.broadcasted_iota(jnp.int32, (vocab, 1), 0)
    transposed = jnp.zeros((table_whole.shape[2], ids_whole.shape[1]), jnp.float32)
    for codebook in range(table_whole.shape[0]):
        picks = (entries == ids_whole[0, :, codebook][None, :]).astype(jnp.bfloat16)
        transposed = transposed + lax.dot_general(
            table_whole[codebook], picks, (((0,), (0,)), ((), ())),
            preferred_element_type=jnp.float32,
        )
    ctx_count = lax.axis_size("ctx")
    transposed = transposed.astype(jnp.bfloat16).reshape(transposed.shape[0], ctx_count, frames_dev)
    gathered = lax.all_to_all(transposed, "ctx", split_axis=1, concat_axis=0, tiled=True)
    embedded = gathered.reshape(-1, frames_dev).T[None]
    weight_qkv, weight_out = (
        lax.all_gather(w_qkv, "dp", axis=0, tiled=True),
        lax.all_gather(w_out, "dp", axis=0, tiled=True),
    )
    model_width = weight_out.shape[0]
    head_size = model_width // head_count
    score_scale = head_size ** (-0.5)
    features = embedded.astype(jnp.float32).reshape(-1, model_width)
    attn_inverse = inverse_rms(features)
    normed = (features * attn_inverse * attn_gain).astype(jnp.bfloat16)
    projected = jnp.dot(normed, weight_qkv, preferred_element_type=jnp.float32).astype(jnp.bfloat16)
    projected = projected.reshape(recordings, frames_dev, 3 * model_width)
    ctx_index = lax.axis_index("ctx")
    back_row = lax.dynamic_index_in_dim(back_list, ctx_index, 0, keepdims=False)
    ahead_row = lax.dynamic_index_in_dim(ahead_list, ctx_index, 0, keepdims=False)
    offsets = [-(step + 1) for step in range(back_list.shape[1])] + [1]
    listed_items = [jnp.array(True)]
    own_keys = projected[:, :, model_width : 2 * model_width]
    own_values = projected[:, :, 2 * model_width :]
    key_blocks = [own_keys]
    value_blocks = [own_values]
    for offset in offsets:
        list_row = back_row if offset < 0 else ahead_row
        listed_items.append(jnp.any(list_row == ctx_index + offset))
        key_blocks.append(from_behind(own_keys, "ctx", -offset))
    for offset in offsets:
        value_blocks.append(from_behind(own_values, "ctx", -offset))
    listed = jnp.stack(listed_items)
    seen_count = len(key_blocks)
    key_all = jnp.stack(key_blocks, axis=1).reshape(
        recordings, seen_count, frames_dev, head_count, head_size
    )
    value_all = jnp.stack(value_blocks, axis=1).reshape(
        recordings, seen_count, frames_dev, head_count, head_size
    )
    query_all = projected[:, :, :model_width].reshape(recordings, frames_dev, head_count, head_size)

    key_flat = key_all.reshape(recordings, -1, head_count, head_size)
    value_flat = value_all.reshape(recordings, -1, head_count, head_size)
    visible = jnp.repeat(listed, frames_dev)
    scores = jnp.where(
        visible,
        jnp.einsum("rqhd,rkhd->rhqk", query_all, key_flat, preferred_element_type=jnp.float32)
        * score_scale,
        NEGATIVE,
    )
    highest = jnp.max(scores, axis=3, keepdims=True)
    weights = jnp.exp(scores - highest)
    probs = weights / jnp.sum(weights, axis=3, keepdims=True)
    probs_low = probs.astype(jnp.bfloat16)
    mixed = jnp.einsum(
        "rhqk,rkhd->rqhd", probs_low, value_flat, preferred_element_type=jnp.float32
    ).astype(jnp.bfloat16)
    mixed = mixed.reshape(recordings * frames_dev, model_width)
    normed_all, mixed = lax.optimization_barrier(
        (lax.all_gather(normed, "dp", axis=0, tiled=True), mixed)
    )
    projection = jnp.dot(mixed, weight_out, preferred_element_type=jnp.float32)
    middle = (features + projection).astype(jnp.bfloat16)
    middle_wide = middle.astype(jnp.float32)
    conv_inverse = inverse_rms(middle_wide)
    conv_input = (
        (middle_wide * conv_inverse * conv_gain)
        .astype(jnp.bfloat16)
        .reshape(recordings, frames_dev, model_width)
    )
    padded = with_halo(conv_input, (("ctx", 1),), rim_width).astype(jnp.float32)

    conv_sum = jnp.zeros((recordings, frames_dev, model_width), jnp.float32)
    for tap_index in range(tap_count):
        conv_sum = conv_sum + conv_kernel[tap_index] * padded[:, tap_index : tap_index + frames_dev]
    middle_frames = middle_wide.reshape(recordings, frames_dev, model_width)
    block_out = (middle_frames + jax.nn.silu(conv_sum)).astype(jnp.bfloat16)
    upstream = cotangent.astype(jnp.float32)
    grad_conv_low = (upstream * silu_slope(conv_sum)).astype(jnp.bfloat16)
    grad_conv = lax.optimization_barrier(grad_conv_low).astype(jnp.float32)
    grad_padded = with_halo(grad_conv_low, (("ctx", 1),), rim_width).astype(jnp.float32)

    grad_input = jnp.zeros((recordings, frames_dev, model_width), jnp.float32)
    kernel_list = []
    for tap_index in range(tap_count):
        window = padded[:, tap_index : tap_index + frames_dev]
        kernel_list.append(jnp.sum(grad_conv * window, axis=(0, 1)))
        start_row = 2 * rim_width - tap_index
        grad_input = grad_input + conv_kernel[tap_index] * grad_padded[
            :, start_row : start_row + frames_dev
        ]
    kernel_rows = jnp.stack(kernel_list)
    kernel_high = lax.reduce_precision(kernel_rows, exponent_bits=8, mantissa_bits=7)
    kernel_parts = jnp.concatenate(
        [kernel_high.astype(jnp.bfloat16), (kernel_rows - kernel_high).astype(jnp.bfloat16)], axis=0
    )
    grad_middle = (
        upstream.reshape(-1, model_width)
        + norm_back(middle_wide, conv_inverse, conv_gain, grad_input.reshape(-1, model_width))
    ).astype(jnp.bfloat16)
    mixed_all, grad_middle = lax.optimization_barrier(
        (lax.all_gather(mixed, "dp", axis=0, tiled=True), grad_middle)
    )
    contract_rows = (((0,), (0,)), ((), ()))
    contract_columns = (((1,), (1,)), ((), ()))
    grad_mixed = lax.dot_general(
        grad_middle, weight_out, contract_columns, preferred_element_type=jnp.float32
    ).astype(jnp.bfloat16)
    dp_index = lax.axis_index("dp")
    shard_width = model_width // lax.axis_size("dp")
    mixed_columns = lax.dynamic_slice_in_dim(mixed_all, dp_index * shard_width, shard_width, 1)
    middle_rows = lax.all_gather(grad_middle, "dp", axis=0, tiled=True)
    grad_heads = grad_mixed.reshape(recordings, frames_dev, head_count, head_size)

    grad_probs = jnp.einsum(
        "rqhd,rkhd->rhqk", grad_heads, value_flat, preferred_element_type=jnp.float32
    )
    row_sum = jnp.sum(probs * grad_probs, axis=3, keepdims=True)
    grad_scores = lax.optimization_barrier(
        (probs * (grad_probs - row_sum) * score_scale).astype(jnp.bfloat16)
    )
    transposed_dims = (((1,), (2,)), ((0, 2), (0, 1)))
    key_grads = lax.dot_general(
        query_all, grad_scores, transposed_dims, preferred_element_type=jnp.float32
    ).reshape(recordings, model_width, -1)
    value_grads = lax.dot_general(
        grad_heads, probs_low, transposed_dims, preferred_element_type=jnp.float32
    ).reshape(recordings, model_width, -1)
    outgoing = [
        jnp.concatenate(
            [key_grads[:, :, window], value_grads[:, :, window]], axis=1
        ).astype(jnp.bfloat16)
        for window in [
            slice((position + 1) * frames_dev, (position + 2) * frames_dev)
            for position in range(len(offsets))
        ]
    ]
    outgoing, scores_for_query = lax.optimization_barrier((outgoing, grad_scores))
    arrivals = [from_behind(sent, "ctx", offset) for sent, offset in zip(outgoing, offsets)]
    grad_query = jnp.einsum(
        "rhqk,rkhd->rqhd", scores_for_query, key_flat, preferred_element_type=jnp.float32
    )
    middle_rows, grad_query = lax.optimization_barrier((middle_rows, grad_query))
    grad_wout = lax.dot_general(
        mixed_columns, middle_rows, contract_rows, preferred_element_type=jnp.float32
    )
    grad_query = grad_query.reshape(recordings * frames_dev, model_width).astype(jnp.bfloat16)
    pair_total = jnp.concatenate(
        [key_grads[:, :, :frames_dev], value_grads[:, :, :frames_dev]], axis=1
    )
    for arrived in arrivals:
        pair_total = pair_total + arrived.astype(jnp.float32)
    pair_low = pair_total.astype(jnp.bfloat16)
    normed_columns = lax.dynamic_slice_in_dim(normed_all, dp_index * shard_width, shard_width, 1)
    query_width = grad_query.shape[0]
    query_block = jnp.concatenate([grad_query, kernel_parts], axis=0)
    query_block = jnp.pad(query_block, ((0, (-query_block.shape[0]) % 16), (0, 0)))
    query_gathered = lax.all_gather(query_block[None], "dp", axis=0, tiled=True)
    query_rows = query_gathered[:, :query_width].reshape(-1, model_width)
    kernel_dp = jnp.sum(
        query_gathered[:, query_width : query_width + tap_count].astype(jnp.float32)
        + query_gathered[:, query_width + tap_count : query_width + 2 * tap_count].astype(
            jnp.float32
        ),
        axis=0,
    )
    grad_wq = lax.dot_general(
        normed_columns, query_rows, contract_rows, preferred_element_type=jnp.float32
    )
    pair_rows = lax.all_gather(pair_low, "dp", axis=0, tiled=True)
    grad_wkv = jnp.einsum(
        "nfc,nkf->ck",
        normed_columns.reshape(pair_rows.shape[0], frames_dev, shard_width),
        pair_rows,
        preferred_element_type=jnp.float32,
    )
    grad_normed = lax.dot_general(
        grad_query, weight_qkv[:, :model_width], contract_columns,
        preferred_element_type=jnp.float32,
    ) + jnp.einsum(
        "rkf,ik->rfi", pair_low, weight_qkv[:, model_width:], preferred_element_type=jnp.float32
    ).reshape(recordings * frames_dev, model_width)
    grad_embedded = (
        grad_middle.astype(jnp.float32) + norm_back(features, attn_inverse, attn_gain, grad_normed)
    ).astype(jnp.bfloat16)
    weight_rows = jnp.concatenate([grad_wq, grad_wkv, grad_wout], axis=1)
    row_width = weight_rows.shape[1]
    kernel_padded = jnp.pad(
        kernel_dp, ((0, (-tap_count * model_width) % row_width // model_width), (0, 0))
    )
    summed = lax.psum(
        jnp.concatenate([weight_rows, kernel_padded.reshape(-1, row_width)], axis=0), "ctx"
    )
    shard_rows = weight_rows.shape[0]
    qkv_width = grad_wq.shape[1] + grad_wkv.shape[1]
    grad_qkv = summed[:shard_rows, :qkv_width]
    grad_out = summed[:shard_rows, qkv_width:]
    grad_kernel = summed[shard_rows:].reshape(-1, model_width)[:tap_count]
    return (
        block_out,
        grad_embedded.reshape(recordings, frames_dev, model_width),
        grad_qkv,
        grad_out,
        grad_kernel,
    )


def solution(mesh):
    in_specs = (
        P("dp", "ctx", None),
        P(None, "dp", "ctx"),
        P("dp", None),
        P("dp", None),
        P(),
        P(),
        P(),
        P(),
        P(),
        P("dp", "ctx", None),
    )
    out_specs = (P("dp", "ctx", None), P("dp", "ctx", None), P("dp", None), P("dp", None), P())
    return jax.shard_map(
        on_device, mesh=mesh, in_specs=in_specs, out_specs=out_specs, check_vma=False
    )
```

```python
import jax
import jax.numpy as jnp
from jax import lax
from jax.sharding import PartitionSpec as P

HEADS = 16


EPSILON = 1e-06
NEGATIVE = -1e30


def from_behind(value, axis, steps):
    count = lax.axis_size(axis)
    first, last = (max(0, -steps), min(count, count - steps))
    return lax.ppermute(value, axis, [(source, source + steps) for source in range(first, last)])


def with_halo(block, sides, width):
    for axis, dim in sides:
        count = lax.axis_size(axis)
        forward = [(i, i + 1) for i in range(count - 1)]
        backward = [(target, source) for source, target in forward]
        low = lax.ppermute(
            lax.slice_in_dim(block, block.shape[dim] - width, None, axis=dim), axis, forward
        )
        high = lax.ppermute(lax.slice_in_dim(block, 0, width, axis=dim), axis, backward)
        block = jnp.concatenate([low, block, high], axis=dim)
    return block


def inverse_rms(features):
    return lax.rsqrt(jnp.mean(features * features, axis=-1, keepdims=True) + EPSILON)


def norm_back(features, inverse, gains, upstream):
    inner = jnp.mean(features * gains * upstream, axis=-1, keepdims=True)
    return inverse * gains * upstream - features * inverse * inverse * inverse * inner


def silu_slope(conv_sum):
    sigmoid = jax.nn.sigmoid(conv_sum)
    return sigmoid * (1.0 + conv_sum * (1.0 - sigmoid))


def block_scores(queries, key_block, listed_block, score_scale):
    return jnp.where(
        listed_block,
        jnp.einsum("rqhd,rkhd->rhqk", queries, key_block, preferred_element_type=jnp.float32)
        * score_scale,
        NEGATIVE,
    )


def probabilities(queries, key_part, listed, score_scale):
    pieces = [
        block_scores(queries, key_part[:, position], listed[position], score_scale)
        for position in range(key_part.shape[1])
    ]
    scores = jnp.concatenate(pieces, axis=3)
    highest = jnp.max(scores, axis=3, keepdims=True)
    weights = jnp.exp(scores - highest)
    return weights / jnp.sum(weights, axis=3, keepdims=True)


def on_device(
    ids, tables, w_qkv, w_out, attn_gain, conv_gain, conv_kernel, back_list, ahead_list, cotangent
):
    recordings = ids.shape[0]
    frames_dev = ids.shape[1]
    head_count = HEADS
    tap_count = conv_kernel.shape[0]
    rim_width = (tap_count - 1) // 2
    ids_whole = lax.all_gather(ids, "ctx", axis=1, tiled=True)
    table_whole = lax.all_gather(tables, "dp", axis=1, tiled=True)
    vocab = table_whole.shape[1]
    entries = lax.broadcasted_iota(jnp.int32, (vocab, 1), 0)
    transposed = jnp.zeros((table_whole.shape[2], ids_whole.shape[1]), jnp.float32)
    for codebook in range(table_whole.shape[0]):
        picks = (entries == ids_whole[0, :, codebook][None, :]).astype(jnp.bfloat16)
        transposed = transposed + lax.dot_general(
            table_whole[codebook], picks, (((0,), (0,)), ((), ())),
            preferred_element_type=jnp.float32,
        )
    ctx_count = lax.axis_size("ctx")
    transposed = transposed.astype(jnp.bfloat16).reshape(transposed.shape[0], ctx_count, frames_dev)
    gathered = lax.all_to_all(transposed, "ctx", split_axis=1, concat_axis=0, tiled=True)
    embedded = gathered.reshape(-1, frames_dev).T[None]
    weight_qkv, weight_out = (
        lax.all_gather(w_qkv, "dp", axis=0, tiled=True),
        lax.all_gather(w_out, "dp", axis=0, tiled=True),
    )
    model_width = weight_out.shape[0]
    head_size = model_width // head_count
    score_scale = head_size ** (-0.5)
    features = embedded.astype(jnp.float32).reshape(-1, model_width)
    attn_inverse = inverse_rms(features)
    normed = (features * attn_inverse * attn_gain).astype(jnp.bfloat16)
    projected = jnp.dot(normed, weight_qkv, preferred_element_type=jnp.float32).astype(jnp.bfloat16)
    projected = projected.reshape(recordings, frames_dev, 3 * model_width)
    ctx_index = lax.axis_index("ctx")
    back_row = lax.dynamic_index_in_dim(back_list, ctx_index, 0, keepdims=False)
    ahead_row = lax.dynamic_index_in_dim(ahead_list, ctx_index, 0, keepdims=False)
    offsets = [-(step + 1) for step in range(back_list.shape[1])] + [1]
    listed_items = [jnp.array(True)]
    own_keys = projected[:, :, model_width : 2 * model_width]
    own_values = projected[:, :, 2 * model_width :]
    key_blocks = [own_keys]
    value_blocks = [own_values]
    for offset in offsets:
        list_row = back_row if offset < 0 else ahead_row
        listed_items.append(jnp.any(list_row == ctx_index + offset))
        key_blocks.append(from_behind(own_keys, "ctx", -offset))
    for offset in offsets:
        value_blocks.append(from_behind(own_values, "ctx", -offset))
    listed = jnp.stack(listed_items)
    seen_count = len(key_blocks)
    key_all = jnp.stack(key_blocks, axis=1).reshape(
        recordings, seen_count, frames_dev, head_count, head_size
    )
    value_all = jnp.stack(value_blocks, axis=1).reshape(
        recordings, seen_count, frames_dev, head_count, head_size
    )
    query_all = projected[:, :, :model_width].reshape(recordings, frames_dev, head_count, head_size)

    key_flat = key_all.reshape(recordings, -1, head_count, head_size)
    value_flat = value_all.reshape(recordings, -1, head_count, head_size)
    visible = jnp.repeat(listed, frames_dev)
    scores = jnp.where(
        visible,
        jnp.einsum("rqhd,rkhd->rhqk", query_all, key_flat, preferred_element_type=jnp.float32)
        * score_scale,
        NEGATIVE,
    )
    highest = jnp.max(scores, axis=3, keepdims=True)
    weights = jnp.exp(scores - highest)
    probs = weights / jnp.sum(weights, axis=3, keepdims=True)
    probs_low = probs.astype(jnp.bfloat16)
    mixed = jnp.einsum(
        "rhqk,rkhd->rqhd", probs_low, value_flat, preferred_element_type=jnp.float32
    ).astype(jnp.bfloat16)
    mixed = mixed.reshape(recordings * frames_dev, model_width)
    normed_all, mixed = lax.optimization_barrier(
        (lax.all_gather(normed, "dp", axis=0, tiled=True), mixed)
    )
    projection = jnp.dot(mixed, weight_out, preferred_element_type=jnp.float32)
    middle = (features + projection).astype(jnp.bfloat16)
    middle_wide = middle.astype(jnp.float32)
    conv_inverse = inverse_rms(middle_wide)
    conv_input = (
        (middle_wide * conv_inverse * conv_gain)
        .astype(jnp.bfloat16)
        .reshape(recordings, frames_dev, model_width)
    )
    padded = with_halo(conv_input, (("ctx", 1),), rim_width).astype(jnp.float32)

    conv_sum = jnp.zeros((recordings, frames_dev, model_width), jnp.float32)
    for tap_index in range(tap_count):
        conv_sum = conv_sum + conv_kernel[tap_index] * padded[:, tap_index : tap_index + frames_dev]
    middle_frames = middle_wide.reshape(recordings, frames_dev, model_width)
    block_out = (middle_frames + jax.nn.silu(conv_sum)).astype(jnp.bfloat16)
    upstream = cotangent.astype(jnp.float32)
    grad_conv_low = (upstream * silu_slope(conv_sum)).astype(jnp.bfloat16)
    grad_conv = lax.optimization_barrier(grad_conv_low).astype(jnp.float32)
    grad_padded = with_halo(grad_conv_low, (("ctx", 1),), rim_width).astype(jnp.float32)

    grad_input = jnp.zeros((recordings, frames_dev, model_width), jnp.float32)
    kernel_list = []
    for tap_index in range(tap_count):
        window = padded[:, tap_index : tap_index + frames_dev]
        kernel_list.append(jnp.sum(grad_conv * window, axis=(0, 1)))
        start_row = 2 * rim_width - tap_index
        grad_input = grad_input + conv_kernel[tap_index] * grad_padded[
            :, start_row : start_row + frames_dev
        ]
    kernel_rows = jnp.stack(kernel_list)
    kernel_high = lax.reduce_precision(kernel_rows, exponent_bits=8, mantissa_bits=7)
    kernel_parts = jnp.concatenate(
        [kernel_high.astype(jnp.bfloat16), (kernel_rows - kernel_high).astype(jnp.bfloat16)], axis=0
    )
    grad_middle = (
        upstream.reshape(-1, model_width)
        + norm_back(middle_wide, conv_inverse, conv_gain, grad_input.reshape(-1, model_width))
    ).astype(jnp.bfloat16)
    mixed_all, grad_middle = lax.optimization_barrier(
        (lax.all_gather(mixed, "dp", axis=0, tiled=True), grad_middle)
    )
    contract_rows = (((0,), (0,)), ((), ()))
    contract_columns = (((1,), (1,)), ((), ()))
    grad_mixed = lax.dot_general(
        grad_middle, weight_out, contract_columns, preferred_element_type=jnp.float32
    ).astype(jnp.bfloat16)
    dp_index = lax.axis_index("dp")
    shard_width = model_width // lax.axis_size("dp")
    mixed_columns = lax.dynamic_slice_in_dim(mixed_all, dp_index * shard_width, shard_width, 1)
    middle_rows = lax.all_gather(grad_middle, "dp", axis=0, tiled=True)
    grad_heads = grad_mixed.reshape(recordings, frames_dev, head_count, head_size)

    grad_probs = jnp.einsum(
        "rqhd,rkhd->rhqk", grad_heads, value_flat, preferred_element_type=jnp.float32
    )
    row_sum = jnp.sum(probs * grad_probs, axis=3, keepdims=True)
    grad_scores = lax.optimization_barrier(
        (probs * (grad_probs - row_sum) * score_scale).astype(jnp.bfloat16)
    )
    transposed_dims = (((1,), (2,)), ((0, 2), (0, 1)))
    key_grads = lax.dot_general(
        query_all, grad_scores, transposed_dims, preferred_element_type=jnp.float32
    ).reshape(recordings, model_width, -1)
    value_grads = lax.dot_general(
        grad_heads, probs_low, transposed_dims, preferred_element_type=jnp.float32
    ).reshape(recordings, model_width, -1)
    outgoing = [
        jnp.concatenate(
            [key_grads[:, :, window], value_grads[:, :, window]], axis=1
        ).astype(jnp.bfloat16)
        for window in [
            slice((position + 1) * frames_dev, (position + 2) * frames_dev)
            for position in range(len(offsets))
        ]
    ]
    outgoing, scores_for_query = lax.optimization_barrier((outgoing, grad_scores))
    arrivals = [from_behind(sent, "ctx", offset) for sent, offset in zip(outgoing, offsets)]
    grad_query = jnp.einsum(
        "rhqk,rkhd->rqhd", scores_for_query, key_flat, preferred_element_type=jnp.float32
    )
    middle_rows, grad_query = lax.optimization_barrier((middle_rows, grad_query))
    grad_wout = lax.dot_general(
        mixed_columns, middle_rows, contract_rows, preferred_element_type=jnp.float32
    )
    grad_query = grad_query.reshape(recordings * frames_dev, model_width).astype(jnp.bfloat16)
    pair_total = jnp.concatenate(
        [key_grads[:, :, :frames_dev], value_grads[:, :, :frames_dev]], axis=1
    )
    for arrived in arrivals:
        pair_total = pair_total + arrived.astype(jnp.float32)
    pair_low = pair_total.astype(jnp.bfloat16)
    normed_columns = lax.dynamic_slice_in_dim(normed_all, dp_index * shard_width, shard_width, 1)
    query_width = grad_query.shape[0]
    query_block = jnp.concatenate([grad_query, kernel_parts], axis=0)
    query_block = jnp.pad(query_block, ((0, (-query_block.shape[0]) % 16), (0, 0)))
    query_gathered = lax.all_gather(query_block[None], "dp", axis=0, tiled=True)
    query_rows = query_gathered[:, :query_width].reshape(-1, model_width)
    kernel_dp = jnp.sum(
        query_gathered[:, query_width : query_width + tap_count].astype(jnp.float32)
        + query_gathered[:, query_width + tap_count : query_width + 2 * tap_count].astype(
            jnp.float32
        ),
        axis=0,
    )
    grad_wq = lax.dot_general(
        normed_columns, query_rows, contract_rows, preferred_element_type=jnp.float32
    )
    query_gathered, pair_low = lax.optimization_barrier((query_gathered, pair_low))
    pair_rows = lax.all_gather(pair_low, "dp", axis=0, tiled=True)
    grad_wkv = jnp.einsum(
        "nfc,nkf->ck",
        normed_columns.reshape(pair_rows.shape[0], frames_dev, shard_width),
        pair_rows,
        preferred_element_type=jnp.float32,
    )
    grad_normed = lax.dot_general(
        grad_query, weight_qkv[:, :model_width], contract_columns,
        preferred_element_type=jnp.float32,
    ) + jnp.einsum(
        "rkf,ik->rfi", pair_low, weight_qkv[:, model_width:], preferred_element_type=jnp.float32
    ).reshape(recordings * frames_dev, model_width)
    grad_embedded = (
        grad_middle.astype(jnp.float32) + norm_back(features, attn_inverse, attn_gain, grad_normed)
    ).astype(jnp.bfloat16)
    weight_rows = jnp.concatenate([grad_wq, grad_wkv, grad_wout], axis=1)
    row_width = weight_rows.shape[1]
    kernel_padded = jnp.pad(
        kernel_dp, ((0, (-tap_count * model_width) % row_width // model_width), (0, 0))
    )
    summed = lax.psum(
        jnp.concatenate([weight_rows, kernel_padded.reshape(-1, row_width)], axis=0), "ctx"
    )
    shard_rows = weight_rows.shape[0]
    qkv_width = grad_wq.shape[1] + grad_wkv.shape[1]
    grad_qkv = summed[:shard_rows, :qkv_width]
    grad_out = summed[:shard_rows, qkv_width:]
    grad_kernel = summed[shard_rows:].reshape(-1, model_width)[:tap_count]
    return (
        block_out,
        grad_embedded.reshape(recordings, frames_dev, model_width),
        grad_qkv,
        grad_out,
        grad_kernel,
    )


def solution(mesh):
    in_specs = (
        P("dp", "ctx", None),
        P(None, "dp", "ctx"),
        P("dp", None),
        P("dp", None),
        P(),
        P(),
        P(),
        P(),
        P(),
        P("dp", "ctx", None),
    )
    out_specs = (P("dp", "ctx", None), P("dp", "ctx", None), P("dp", None), P("dp", None), P())
    return jax.shard_map(
        on_device, mesh=mesh, in_specs=in_specs, out_specs=out_specs, check_vma=False
    )
```

```python
import jax
import jax.numpy as jnp
from jax import lax
from jax.sharding import PartitionSpec as P

HEADS = 16


EPSILON = 1e-06
NEGATIVE = -1e30


def from_behind(value, axis, steps):
    count = lax.axis_size(axis)
    first, last = (max(0, -steps), min(count, count - steps))
    return lax.ppermute(value, axis, [(source, source + steps) for source in range(first, last)])


def with_halo(block, sides, width):
    for axis, dim in sides:
        count = lax.axis_size(axis)
        forward = [(i, i + 1) for i in range(count - 1)]
        backward = [(target, source) for source, target in forward]
        low = lax.ppermute(
            lax.slice_in_dim(block, block.shape[dim] - width, None, axis=dim), axis, forward
        )
        high = lax.ppermute(lax.slice_in_dim(block, 0, width, axis=dim), axis, backward)
        block = jnp.concatenate([low, block, high], axis=dim)
    return block


def inverse_rms(features):
    return lax.rsqrt(jnp.mean(features * features, axis=-1, keepdims=True) + EPSILON)


def norm_back(features, inverse, gains, upstream):
    inner = jnp.mean(features * gains * upstream, axis=-1, keepdims=True)
    return inverse * gains * upstream - features * inverse * inverse * inverse * inner


def silu_slope(conv_sum):
    sigmoid = jax.nn.sigmoid(conv_sum)
    return sigmoid * (1.0 + conv_sum * (1.0 - sigmoid))


def block_scores(queries, key_block, listed_block, score_scale):
    return jnp.where(
        listed_block,
        jnp.einsum("rqhd,rkhd->rhqk", queries, key_block, preferred_element_type=jnp.float32)
        * score_scale,
        NEGATIVE,
    )


def probabilities(queries, key_part, listed, score_scale):
    pieces = [
        block_scores(queries, key_part[:, position], listed[position], score_scale)
        for position in range(key_part.shape[1])
    ]
    scores = jnp.concatenate(pieces, axis=3)
    highest = jnp.max(scores, axis=3, keepdims=True)
    weights = jnp.exp(scores - highest)
    return weights / jnp.sum(weights, axis=3, keepdims=True)


def on_device(
    ids, tables, w_qkv, w_out, attn_gain, conv_gain, conv_kernel, back_list, ahead_list, cotangent
):
    recordings = ids.shape[0]
    frames_dev = ids.shape[1]
    head_count = HEADS
    tap_count = conv_kernel.shape[0]
    rim_width = (tap_count - 1) // 2
    ids_whole = lax.all_gather(ids, "ctx", axis=1, tiled=True)
    table_whole = lax.all_gather(tables, "dp", axis=1, tiled=True)
    vocab = table_whole.shape[1]
    entries = lax.broadcasted_iota(jnp.int32, (vocab, 1), 0)
    transposed = jnp.zeros((table_whole.shape[2], ids_whole.shape[1]), jnp.float32)
    for codebook in range(table_whole.shape[0]):
        picks = (entries == ids_whole[0, :, codebook][None, :]).astype(jnp.bfloat16)
        transposed = transposed + lax.dot_general(
            table_whole[codebook], picks, (((0,), (0,)), ((), ())),
            preferred_element_type=jnp.float32,
        )
    ctx_count = lax.axis_size("ctx")
    transposed = transposed.astype(jnp.bfloat16).reshape(transposed.shape[0], ctx_count, frames_dev)
    gathered = lax.all_to_all(transposed, "ctx", split_axis=1, concat_axis=0, tiled=True)
    embedded = gathered.reshape(-1, frames_dev).T[None]
    weight_qkv, weight_out = (
        lax.all_gather(w_qkv, "dp", axis=0, tiled=True),
        lax.all_gather(w_out, "dp", axis=0, tiled=True),
    )
    model_width = weight_out.shape[0]
    head_size = model_width // head_count
    score_scale = head_size ** (-0.5)
    features = embedded.astype(jnp.float32).reshape(-1, model_width)
    attn_inverse = inverse_rms(features)
    normed = (features * attn_inverse * attn_gain).astype(jnp.bfloat16)
    projected = jnp.dot(normed, weight_qkv, preferred_element_type=jnp.float32).astype(jnp.bfloat16)
    projected = projected.reshape(recordings, frames_dev, 3 * model_width)
    ctx_index = lax.axis_index("ctx")
    back_row = lax.dynamic_index_in_dim(back_list, ctx_index, 0, keepdims=False)
    ahead_row = lax.dynamic_index_in_dim(ahead_list, ctx_index, 0, keepdims=False)
    offsets = [-(step + 1) for step in range(back_list.shape[1])] + [1]
    listed_items = [jnp.array(True)]
    own_keys = projected[:, :, model_width : 2 * model_width]
    own_values = projected[:, :, 2 * model_width :]
    key_blocks = [own_keys]
    value_blocks = [own_values]
    for offset in offsets:
        list_row = back_row if offset < 0 else ahead_row
        listed_items.append(jnp.any(list_row == ctx_index + offset))
        key_blocks.append(from_behind(own_keys, "ctx", -offset))
    for offset in offsets:
        value_blocks.append(from_behind(own_values, "ctx", -offset))
    listed = jnp.stack(listed_items)
    seen_count = len(key_blocks)
    key_all = jnp.stack(key_blocks, axis=1).reshape(
        recordings, seen_count, frames_dev, head_count, head_size
    )
    value_all = jnp.stack(value_blocks, axis=1).reshape(
        recordings, seen_count, frames_dev, head_count, head_size
    )
    query_all = projected[:, :, :model_width].reshape(recordings, frames_dev, head_count, head_size)

    key_flat = key_all.reshape(recordings, -1, head_count, head_size)
    value_flat = value_all.reshape(recordings, -1, head_count, head_size)
    visible = jnp.repeat(listed, frames_dev)
    scores = jnp.where(
        visible,
        jnp.einsum("rqhd,rkhd->rhqk", query_all, key_flat, preferred_element_type=jnp.float32)
        * score_scale,
        NEGATIVE,
    )
    highest = jnp.max(scores, axis=3, keepdims=True)
    weights = jnp.exp(scores - highest)
    probs = weights / jnp.sum(weights, axis=3, keepdims=True)
    probs_low = probs.astype(jnp.bfloat16)
    mixed = jnp.einsum(
        "rhqk,rkhd->rqhd", probs_low, value_flat, preferred_element_type=jnp.float32
    ).astype(jnp.bfloat16)
    mixed = mixed.reshape(recordings * frames_dev, model_width)
    normed_all, mixed = lax.optimization_barrier(
        (lax.all_gather(normed, "dp", axis=0, tiled=True), mixed)
    )
    projection = jnp.dot(mixed, weight_out, preferred_element_type=jnp.float32)
    middle = (features + projection).astype(jnp.bfloat16)
    middle_wide = middle.astype(jnp.float32)
    conv_inverse = inverse_rms(middle_wide)
    conv_input = (
        (middle_wide * conv_inverse * conv_gain)
        .astype(jnp.bfloat16)
        .reshape(recordings, frames_dev, model_width)
    )
    padded = with_halo(conv_input, (("ctx", 1),), rim_width).astype(jnp.float32)

    conv_sum = jnp.zeros((recordings, frames_dev, model_width), jnp.float32)
    for tap_index in range(tap_count):
        conv_sum = conv_sum + conv_kernel[tap_index] * padded[:, tap_index : tap_index + frames_dev]
    middle_frames = middle_wide.reshape(recordings, frames_dev, model_width)
    block_out = (middle_frames + jax.nn.silu(conv_sum)).astype(jnp.bfloat16)
    upstream = cotangent.astype(jnp.float32)
    grad_conv_low = (upstream * silu_slope(conv_sum)).astype(jnp.bfloat16)
    grad_conv = lax.optimization_barrier(grad_conv_low).astype(jnp.float32)
    grad_padded = with_halo(grad_conv_low, (("ctx", 1),), rim_width).astype(jnp.float32)

    grad_input = jnp.zeros((recordings, frames_dev, model_width), jnp.float32)
    kernel_list = []
    for tap_index in range(tap_count):
        window = padded[:, tap_index : tap_index + frames_dev]
        kernel_list.append(jnp.sum(grad_conv * window, axis=(0, 1)))
        start_row = 2 * rim_width - tap_index
        grad_input = grad_input + conv_kernel[tap_index] * grad_padded[
            :, start_row : start_row + frames_dev
        ]
    kernel_rows = jnp.stack(kernel_list)
    kernel_high = lax.reduce_precision(kernel_rows, exponent_bits=8, mantissa_bits=7)
    kernel_parts = jnp.concatenate(
        [kernel_high.astype(jnp.bfloat16), (kernel_rows - kernel_high).astype(jnp.bfloat16)], axis=0
    )
    grad_middle = (
        upstream.reshape(-1, model_width)
        + norm_back(middle_wide, conv_inverse, conv_gain, grad_input.reshape(-1, model_width))
    ).astype(jnp.bfloat16)
    mixed_all, grad_middle = lax.optimization_barrier(
        (lax.all_gather(mixed, "dp", axis=0, tiled=True), grad_middle)
    )
    contract_rows = (((0,), (0,)), ((), ()))
    contract_columns = (((1,), (1,)), ((), ()))
    grad_mixed = lax.dot_general(
        grad_middle, weight_out, contract_columns, preferred_element_type=jnp.float32
    ).astype(jnp.bfloat16)
    dp_index = lax.axis_index("dp")
    shard_width = model_width // lax.axis_size("dp")
    mixed_columns = lax.dynamic_slice_in_dim(mixed_all, dp_index * shard_width, shard_width, 1)
    middle_rows = lax.all_gather(grad_middle, "dp", axis=0, tiled=True)
    grad_heads = grad_mixed.reshape(recordings, frames_dev, head_count, head_size)

    transposed_dims = (((1,), (2,)), ((0, 2), (0, 1)))
    value_grads = lax.dot_general(
        grad_heads, probs_low, transposed_dims, preferred_element_type=jnp.float32
    ).reshape(recordings, model_width, -1)
    windows = [
        slice((position + 1) * frames_dev, (position + 2) * frames_dev)
        for position in range(len(offsets))
    ]
    value_out = [value_grads[:, :, window].astype(jnp.bfloat16) for window in windows]
    value_arrivals = [from_behind(sent, "ctx", offset) for sent, offset in zip(value_out, offsets)]
    value_arrivals, probs_back = lax.optimization_barrier((value_arrivals, probs))
    grad_probs = jnp.einsum(
        "rqhd,rkhd->rhqk", grad_heads, value_flat, preferred_element_type=jnp.float32
    )
    row_sum = jnp.sum(probs_back * grad_probs, axis=3, keepdims=True)
    grad_scores = lax.optimization_barrier(
        (probs_back * (grad_probs - row_sum) * score_scale).astype(jnp.bfloat16)
    )
    key_grads = lax.dot_general(
        query_all, grad_scores, transposed_dims, preferred_element_type=jnp.float32
    ).reshape(recordings, model_width, -1)
    outgoing = [key_grads[:, :, window].astype(jnp.bfloat16) for window in windows]
    outgoing, scores_for_query = lax.optimization_barrier((outgoing, grad_scores))
    arrivals = [from_behind(sent, "ctx", offset) for sent, offset in zip(outgoing, offsets)]
    grad_query = jnp.einsum(
        "rhqk,rkhd->rqhd", scores_for_query, key_flat, preferred_element_type=jnp.float32
    )
    middle_rows, grad_query = lax.optimization_barrier((middle_rows, grad_query))
    grad_wout = lax.dot_general(
        mixed_columns, middle_rows, contract_rows, preferred_element_type=jnp.float32
    )
    grad_query = grad_query.reshape(recordings * frames_dev, model_width).astype(jnp.bfloat16)
    key_total = key_grads[:, :, :frames_dev]
    value_total = value_grads[:, :, :frames_dev]
    for key_arrived, value_arrived in zip(arrivals, value_arrivals):
        key_total = key_total + key_arrived.astype(jnp.float32)
        value_total = value_total + value_arrived.astype(jnp.float32)
    pair_total = jnp.concatenate([key_total, value_total], axis=1)
    pair_low = pair_total.astype(jnp.bfloat16)
    normed_columns = lax.dynamic_slice_in_dim(normed_all, dp_index * shard_width, shard_width, 1)
    query_width = grad_query.shape[0]
    query_block = jnp.concatenate([grad_query, kernel_parts], axis=0)
    query_block = jnp.pad(query_block, ((0, (-query_block.shape[0]) % 16), (0, 0)))
    query_gathered = lax.all_gather(query_block[None], "dp", axis=0, tiled=True)
    query_rows = query_gathered[:, :query_width].reshape(-1, model_width)
    kernel_dp = jnp.sum(
        query_gathered[:, query_width : query_width + tap_count].astype(jnp.float32)
        + query_gathered[:, query_width + tap_count : query_width + 2 * tap_count].astype(
            jnp.float32
        ),
        axis=0,
    )
    grad_wq = lax.dot_general(
        normed_columns, query_rows, contract_rows, preferred_element_type=jnp.float32
    )
    query_gathered, pair_low = lax.optimization_barrier((query_gathered, pair_low))
    pair_rows = lax.all_gather(pair_low, "dp", axis=0, tiled=True)
    grad_wkv = jnp.einsum(
        "nfc,nkf->ck",
        normed_columns.reshape(pair_rows.shape[0], frames_dev, shard_width),
        pair_rows,
        preferred_element_type=jnp.float32,
    )
    grad_normed = lax.dot_general(
        grad_query, weight_qkv[:, :model_width], contract_columns,
        preferred_element_type=jnp.float32,
    ) + jnp.einsum(
        "rkf,ik->rfi", pair_low, weight_qkv[:, model_width:], preferred_element_type=jnp.float32
    ).reshape(recordings * frames_dev, model_width)
    grad_embedded = (
        grad_middle.astype(jnp.float32) + norm_back(features, attn_inverse, attn_gain, grad_normed)
    ).astype(jnp.bfloat16)
    weight_rows = jnp.concatenate([grad_wq, grad_wkv, grad_wout], axis=1)
    row_width = weight_rows.shape[1]
    kernel_padded = jnp.pad(
        kernel_dp, ((0, (-tap_count * model_width) % row_width // model_width), (0, 0))
    )
    summed = lax.psum(
        jnp.concatenate([weight_rows, kernel_padded.reshape(-1, row_width)], axis=0), "ctx"
    )
    shard_rows = weight_rows.shape[0]
    qkv_width = grad_wq.shape[1] + grad_wkv.shape[1]
    grad_qkv = summed[:shard_rows, :qkv_width]
    grad_out = summed[:shard_rows, qkv_width:]
    grad_kernel = summed[shard_rows:].reshape(-1, model_width)[:tap_count]
    return (
        block_out,
        grad_embedded.reshape(recordings, frames_dev, model_width),
        grad_qkv,
        grad_out,
        grad_kernel,
    )


def solution(mesh):
    in_specs = (
        P("dp", "ctx", None),
        P(None, "dp", "ctx"),
        P("dp", None),
        P("dp", None),
        P(),
        P(),
        P(),
        P(),
        P(),
        P("dp", "ctx", None),
    )
    out_specs = (P("dp", "ctx", None), P("dp", "ctx", None), P("dp", None), P("dp", None), P())
    return jax.shard_map(
        on_device, mesh=mesh, in_specs=in_specs, out_specs=out_specs, check_vma=False
    )
```

```python
import jax
import jax.numpy as jnp
from jax import lax
from jax.sharding import PartitionSpec as P

HEADS = 16


EPSILON = 1e-06
NEGATIVE = -1e30


def from_behind(value, axis, steps):
    count = lax.axis_size(axis)
    first, last = (max(0, -steps), min(count, count - steps))
    return lax.ppermute(value, axis, [(source, source + steps) for source in range(first, last)])


def with_halo(block, sides, width):
    for axis, dim in sides:
        count = lax.axis_size(axis)
        forward = [(i, i + 1) for i in range(count - 1)]
        backward = [(target, source) for source, target in forward]
        low = lax.ppermute(
            lax.slice_in_dim(block, block.shape[dim] - width, None, axis=dim), axis, forward
        )
        high = lax.ppermute(lax.slice_in_dim(block, 0, width, axis=dim), axis, backward)
        block = jnp.concatenate([low, block, high], axis=dim)
    return block


def inverse_rms(features):
    return lax.rsqrt(jnp.mean(features * features, axis=-1, keepdims=True) + EPSILON)


def norm_back(features, inverse, gains, upstream):
    inner = jnp.mean(features * gains * upstream, axis=-1, keepdims=True)
    return inverse * gains * upstream - features * inverse * inverse * inverse * inner


def silu_slope(conv_sum):
    sigmoid = jax.nn.sigmoid(conv_sum)
    return sigmoid * (1.0 + conv_sum * (1.0 - sigmoid))


def block_scores(queries, key_block, listed_block, score_scale):
    return jnp.where(
        listed_block,
        jnp.einsum("rqhd,rkhd->rhqk", queries, key_block, preferred_element_type=jnp.float32)
        * score_scale,
        NEGATIVE,
    )


def probabilities(queries, key_part, listed, score_scale):
    pieces = [
        block_scores(queries, key_part[:, position], listed[position], score_scale)
        for position in range(key_part.shape[1])
    ]
    scores = jnp.concatenate(pieces, axis=3)
    highest = jnp.max(scores, axis=3, keepdims=True)
    weights = jnp.exp(scores - highest)
    return weights / jnp.sum(weights, axis=3, keepdims=True)


def on_device(
    ids, tables, w_qkv, w_out, attn_gain, conv_gain, conv_kernel, back_list, ahead_list, cotangent
):
    recordings = ids.shape[0]
    frames_dev = ids.shape[1]
    head_count = HEADS
    tap_count = conv_kernel.shape[0]
    rim_width = (tap_count - 1) // 2
    ids_whole = lax.all_gather(ids, "ctx", axis=1, tiled=True)
    table_whole = lax.all_gather(tables, "dp", axis=1, tiled=True)
    vocab = table_whole.shape[1]
    entries = lax.broadcasted_iota(jnp.int32, (vocab, 1), 0)
    transposed = jnp.zeros((table_whole.shape[2], ids_whole.shape[1]), jnp.float32)
    for codebook in range(table_whole.shape[0]):
        picks = (entries == ids_whole[0, :, codebook][None, :]).astype(jnp.bfloat16)
        transposed = transposed + lax.dot_general(
            table_whole[codebook], picks, (((0,), (0,)), ((), ())),
            preferred_element_type=jnp.float32,
        )
    ctx_count = lax.axis_size("ctx")
    transposed = transposed.astype(jnp.bfloat16).reshape(transposed.shape[0], ctx_count, frames_dev)
    gathered = lax.all_to_all(transposed, "ctx", split_axis=1, concat_axis=0, tiled=True)
    embedded = gathered.reshape(-1, frames_dev).T[None]
    weight_qkv, weight_out = (
        lax.all_gather(w_qkv, "dp", axis=0, tiled=True),
        lax.all_gather(w_out, "dp", axis=0, tiled=True),
    )
    model_width = weight_out.shape[0]
    head_size = model_width // head_count
    score_scale = head_size ** (-0.5)
    features = embedded.astype(jnp.float32).reshape(-1, model_width)
    attn_inverse = inverse_rms(features)
    normed = (features * attn_inverse * attn_gain).astype(jnp.bfloat16)
    pairs = jnp.dot(
        normed, weight_qkv[:, model_width:], preferred_element_type=jnp.float32
    ).astype(jnp.bfloat16).reshape(recordings, frames_dev, 2 * model_width)
    ctx_index = lax.axis_index("ctx")
    back_row = lax.dynamic_index_in_dim(back_list, ctx_index, 0, keepdims=False)
    ahead_row = lax.dynamic_index_in_dim(ahead_list, ctx_index, 0, keepdims=False)
    offsets = [-(step + 1) for step in range(back_list.shape[1])] + [1]
    listed_items = [jnp.array(True)]
    own_keys = pairs[:, :, :model_width]
    own_values = pairs[:, :, model_width:]
    key_blocks = [own_keys]
    value_blocks = [own_values]
    for offset in offsets:
        list_row = back_row if offset < 0 else ahead_row
        listed_items.append(jnp.any(list_row == ctx_index + offset))
        key_blocks.append(from_behind(own_keys, "ctx", -offset))
    for offset in offsets:
        value_blocks.append(from_behind(own_values, "ctx", -offset))
    listed = jnp.stack(listed_items)
    seen_count = len(key_blocks)
    key_all = jnp.stack(key_blocks, axis=1).reshape(
        recordings, seen_count, frames_dev, head_count, head_size
    )
    value_all = jnp.stack(value_blocks, axis=1).reshape(
        recordings, seen_count, frames_dev, head_count, head_size
    )
    query_all = jnp.dot(
        normed, weight_qkv[:, :model_width], preferred_element_type=jnp.float32
    ).astype(jnp.bfloat16).reshape(recordings, frames_dev, head_count, head_size)

    key_flat = key_all.reshape(recordings, -1, head_count, head_size)
    value_flat = value_all.reshape(recordings, -1, head_count, head_size)
    visible = jnp.repeat(listed, frames_dev)
    scores = jnp.where(
        visible,
        jnp.einsum("rqhd,rkhd->rhqk", query_all, key_flat, preferred_element_type=jnp.float32)
        * score_scale,
        NEGATIVE,
    )
    highest = jnp.max(scores, axis=3, keepdims=True)
    weights = jnp.exp(scores - highest)
    probs = weights / jnp.sum(weights, axis=3, keepdims=True)
    probs_low = probs.astype(jnp.bfloat16)
    mixed = jnp.einsum(
        "rhqk,rkhd->rqhd", probs_low, value_flat, preferred_element_type=jnp.float32
    ).astype(jnp.bfloat16)
    mixed = mixed.reshape(recordings * frames_dev, model_width)
    normed_all, mixed = lax.optimization_barrier(
        (lax.all_gather(normed, "dp", axis=0, tiled=True), mixed)
    )
    projection = jnp.dot(mixed, weight_out, preferred_element_type=jnp.float32)
    middle = (features + projection).astype(jnp.bfloat16)
    middle_wide = middle.astype(jnp.float32)
    conv_inverse = inverse_rms(middle_wide)
    conv_input = (
        (middle_wide * conv_inverse * conv_gain)
        .astype(jnp.bfloat16)
        .reshape(recordings, frames_dev, model_width)
    )
    padded = with_halo(conv_input, (("ctx", 1),), rim_width).astype(jnp.float32)

    conv_sum = jnp.zeros((recordings, frames_dev, model_width), jnp.float32)
    for tap_index in range(tap_count):
        conv_sum = conv_sum + conv_kernel[tap_index] * padded[:, tap_index : tap_index + frames_dev]
    middle_frames = middle_wide.reshape(recordings, frames_dev, model_width)
    block_out = (middle_frames + jax.nn.silu(conv_sum)).astype(jnp.bfloat16)
    upstream = cotangent.astype(jnp.float32)
    grad_conv_low = (upstream * silu_slope(conv_sum)).astype(jnp.bfloat16)
    grad_conv = lax.optimization_barrier(grad_conv_low).astype(jnp.float32)
    grad_padded = with_halo(grad_conv_low, (("ctx", 1),), rim_width).astype(jnp.float32)

    grad_input = jnp.zeros((recordings, frames_dev, model_width), jnp.float32)
    kernel_list = []
    for tap_index in range(tap_count):
        window = padded[:, tap_index : tap_index + frames_dev]
        kernel_list.append(jnp.sum(grad_conv * window, axis=(0, 1)))
        start_row = 2 * rim_width - tap_index
        grad_input = grad_input + conv_kernel[tap_index] * grad_padded[
            :, start_row : start_row + frames_dev
        ]
    kernel_rows = jnp.stack(kernel_list)
    kernel_high = lax.reduce_precision(kernel_rows, exponent_bits=8, mantissa_bits=7)
    kernel_parts = jnp.concatenate(
        [kernel_high.astype(jnp.bfloat16), (kernel_rows - kernel_high).astype(jnp.bfloat16)], axis=0
    )
    grad_middle = (
        upstream.reshape(-1, model_width)
        + norm_back(middle_wide, conv_inverse, conv_gain, grad_input.reshape(-1, model_width))
    ).astype(jnp.bfloat16)
    mixed_all, grad_middle = lax.optimization_barrier(
        (lax.all_gather(mixed, "dp", axis=0, tiled=True), grad_middle)
    )
    contract_rows = (((0,), (0,)), ((), ()))
    contract_columns = (((1,), (1,)), ((), ()))
    grad_mixed = lax.dot_general(
        grad_middle, weight_out, contract_columns, preferred_element_type=jnp.float32
    ).astype(jnp.bfloat16)
    dp_index = lax.axis_index("dp")
    shard_width = model_width // lax.axis_size("dp")
    mixed_columns = lax.dynamic_slice_in_dim(mixed_all, dp_index * shard_width, shard_width, 1)
    middle_rows = lax.all_gather(grad_middle, "dp", axis=0, tiled=True)
    grad_heads = grad_mixed.reshape(recordings, frames_dev, head_count, head_size)

    grad_probs = jnp.einsum(
        "rqhd,rkhd->rhqk", grad_heads, value_flat, preferred_element_type=jnp.float32
    )
    row_sum = jnp.sum(probs * grad_probs, axis=3, keepdims=True)
    grad_scores = lax.optimization_barrier(
        (probs * (grad_probs - row_sum) * score_scale).astype(jnp.bfloat16)
    )
    transposed_dims = (((1,), (2,)), ((0, 2), (0, 1)))
    key_grads = lax.dot_general(
        query_all, grad_scores, transposed_dims, preferred_element_type=jnp.float32
    ).reshape(recordings, model_width, -1)
    value_grads = lax.dot_general(
        grad_heads, probs_low, transposed_dims, preferred_element_type=jnp.float32
    ).reshape(recordings, model_width, -1)
    outgoing = [
        jnp.concatenate(
            [key_grads[:, :, window], value_grads[:, :, window]], axis=1
        ).astype(jnp.bfloat16)
        for window in [
            slice((position + 1) * frames_dev, (position + 2) * frames_dev)
            for position in range(len(offsets))
        ]
    ]
    outgoing, scores_for_query = lax.optimization_barrier((outgoing, grad_scores))
    arrivals = [from_behind(sent, "ctx", offset) for sent, offset in zip(outgoing, offsets)]
    grad_query = jnp.einsum(
        "rhqk,rkhd->rqhd", scores_for_query, key_flat, preferred_element_type=jnp.float32
    )
    middle_rows, grad_query = lax.optimization_barrier((middle_rows, grad_query))
    grad_wout = lax.dot_general(
        mixed_columns, middle_rows, contract_rows, preferred_element_type=jnp.float32
    )
    grad_query = grad_query.reshape(recordings * frames_dev, model_width).astype(jnp.bfloat16)
    pair_total = jnp.concatenate(
        [key_grads[:, :, :frames_dev], value_grads[:, :, :frames_dev]], axis=1
    )
    for arrived in arrivals:
        pair_total = pair_total + arrived.astype(jnp.float32)
    pair_low = pair_total.astype(jnp.bfloat16)
    normed_columns = lax.dynamic_slice_in_dim(normed_all, dp_index * shard_width, shard_width, 1)
    query_width = grad_query.shape[0]
    query_block = jnp.concatenate([grad_query, kernel_parts], axis=0)
    query_block = jnp.pad(query_block, ((0, (-query_block.shape[0]) % 16), (0, 0)))
    query_gathered = lax.all_gather(query_block[None], "dp", axis=0, tiled=True)
    query_rows = query_gathered[:, :query_width].reshape(-1, model_width)
    kernel_dp = jnp.sum(
        query_gathered[:, query_width : query_width + tap_count].astype(jnp.float32)
        + query_gathered[:, query_width + tap_count : query_width + 2 * tap_count].astype(
            jnp.float32
        ),
        axis=0,
    )
    grad_wq = lax.dot_general(
        normed_columns, query_rows, contract_rows, preferred_element_type=jnp.float32
    )
    query_gathered, pair_low = lax.optimization_barrier((query_gathered, pair_low))
    pair_rows = lax.all_gather(pair_low, "dp", axis=0, tiled=True)
    grad_wkv = jnp.einsum(
        "nfc,nkf->ck",
        normed_columns.reshape(pair_rows.shape[0], frames_dev, shard_width),
        pair_rows,
        preferred_element_type=jnp.float32,
    )
    grad_normed = lax.dot_general(
        grad_query, weight_qkv[:, :model_width], contract_columns,
        preferred_element_type=jnp.float32,
    ) + jnp.einsum(
        "rkf,ik->rfi", pair_low, weight_qkv[:, model_width:], preferred_element_type=jnp.float32
    ).reshape(recordings * frames_dev, model_width)
    grad_embedded = (
        grad_middle.astype(jnp.float32) + norm_back(features, attn_inverse, attn_gain, grad_normed)
    ).astype(jnp.bfloat16)
    weight_rows = jnp.concatenate([grad_wq, grad_wkv, grad_wout], axis=1)
    row_width = weight_rows.shape[1]
    kernel_padded = jnp.pad(
        kernel_dp, ((0, (-tap_count * model_width) % row_width // model_width), (0, 0))
    )
    summed = lax.psum(
        jnp.concatenate([weight_rows, kernel_padded.reshape(-1, row_width)], axis=0), "ctx"
    )
    shard_rows = weight_rows.shape[0]
    qkv_width = grad_wq.shape[1] + grad_wkv.shape[1]
    grad_qkv = summed[:shard_rows, :qkv_width]
    grad_out = summed[:shard_rows, qkv_width:]
    grad_kernel = summed[shard_rows:].reshape(-1, model_width)[:tap_count]
    return (
        block_out,
        grad_embedded.reshape(recordings, frames_dev, model_width),
        grad_qkv,
        grad_out,
        grad_kernel,
    )


def solution(mesh):
    in_specs = (
        P("dp", "ctx", None),
        P(None, "dp", "ctx"),
        P("dp", None),
        P("dp", None),
        P(),
        P(),
        P(),
        P(),
        P(),
        P("dp", "ctx", None),
    )
    out_specs = (P("dp", "ctx", None), P("dp", "ctx", None), P("dp", None), P("dp", None), P())
    return jax.shard_map(
        on_device, mesh=mesh, in_specs=in_specs, out_specs=out_specs, check_vma=False
    )
```
